512 devices in a mesh: seq: 64 (over y, x, z_hi), head: 8 (over z_lo, core).
Axes of the slice: x: 4, y: 8, z: 8 (z_hi: 2, z_lo: 4; z = z_hi * 4 + z_lo), core: 2. Of those that a mesh axis runs over, the one named last changes fastest.
Arguments:
- queries: bfloat16 [32768, 16, 128], P('seq', 'head'), may hold values from -6 to 6
- keys: bfloat16 [32768, 16, 128], P('seq', 'head'), may hold values from -6 to 6
- values: bfloat16 [32768, 16, 128], P('seq', 'head'), may hold values from -6 to 6
- clusters: int32 [16, 32768, 1], P('head', 'seq'), may hold values from 0 to 255; in each aligned block of 512 rows (0 to 511, 512 to 1023, ..., all dimensions but the last counted through in order) at most 8 rows name the same one
- cent_keys: bfloat16 [16, 256, 128], P('head', 'seq'), may hold values from -6 to 6
- cent_values: bfloat16 [16, 256, 128], P('head', 'seq'), may hold values from -6 to 6
- out_weight: bfloat16 [2048, 4096], P('head'), may hold values from -0.1875 to 0.1875
Outputs:
- mixed: bfloat16 [4096, 32768], P('head', 'seq')
The draws below stay inside these ranges and needn't reach their ends.
Inputs may be any that keep to these rules, and one draw needn't show every extreme that they name: `clusters`: among the 512 tokens of one device in one head (an aligned block of rows), no cluster is named more than 8 times; in some such block a cluster is named exactly 8 times.
All inputs are finite; a program needn't handle non-finite values.
Results may differ from the reference program's by a relative error of at most 0.017.
Values may be sent and summed in bfloat16 or wider, within the bound.
No kernel may reach another device: no remote copies, remote signals or barrier semaphores. Data moves between devices by JAX's collectives and lax.ppermute only.
A program may use at most 128 MiB of HBM per device.

```python
import math
import jax
import jax.numpy as jnp
import numpy as np
from jax import lax

D = 4096
HEADS = 16
HD = 128
CLUSTERS = 256
MOST = 8
TOK_DEV = 512
TOKENS = 32768
N_SEQ = 64
N_HEAD = 8


def draw_queries(key, part):
    subkey = jax.random.fold_in(key, 11)
    shape = (TOKENS, HEADS, HD)
    base = jnp.clip(jax.random.normal(subkey, shape, jnp.float32), -6.0, 6.0)
    return base.astype(jnp.bfloat16)


def draw_cent_keys(key, part):
    subkey = jax.random.fold_in(key, 23)
    shape = (HEADS, CLUSTERS, HD)
    base = jnp.clip(jax.random.normal(subkey, shape, jnp.float32), -6.0, 6.0)
    return base.astype(jnp.bfloat16)


def raised(values, key, source, target, blocks, factor):
    def block_of(dim):
        return (jnp.arange(values.shape[dim]) // (values.shape[dim] // blocks)).reshape((-1,) + (1,) * (values.ndim - 1 - dim))

    near = jax.random.permutation(key, blocks)[block_of(target)]
    far = (block_of(target) + blocks // 2) % blocks
    return jnp.where((block_of(source) == near) | (block_of(source) == far), factor * values, values)


def block_scale(key, dims, cuts, low, top_value):
    level, own = 1.0, jax.random.fold_in(key, 6)
    for dim, shards_of in cuts:
        draws = jnp.exp(jax.random.uniform(jax.random.fold_in(own, dim), (shards_of,), jnp.float32, low / len(cuts), top_value / len(cuts)))
        level = level * jnp.repeat(draws, dims[dim] // shards_of).reshape([-1 if axis == dim else 1 for axis in range(len(dims))])
    return level


def deal_out(rng, own, number, rows, count, top, limit, slope):
    order = jax.random.permutation(rng, count)
    packed, ordinary = shares(count, rows * top, limit, slope, True), shares(count, rows * top, limit, slope, False)
    places = jnp.arange(count)

    def named(sizes, turn):
        used = int((sizes > 0).sum())
        fixed = max(1, used // 4)
        passed = fixed + (places - fixed + turn * (used - fixed)) % max(1, count - fixed)
        return jnp.zeros((count,), jnp.int32).at[order[jnp.where(places < fixed, places, passed)]].set(jnp.asarray(sizes, jnp.int32))

    sizes = jnp.where(number % 4 == 0, named(packed, number // 4), named(ordinary, number - number // 4 - 1))
    mixed = jax.random.permutation(jax.random.fold_in(own, 3), count)
    source_of, taker = mixed[0:count // 2 * 2:2], mixed[1:count // 2 * 2:2]
    slack = jnp.minimum(sizes[source_of] - 1, limit - sizes[taker]) // 2
    slack = jnp.where((source_of == order[0]) | (taker == order[0]) | (sizes[taker] == 0), 0, jnp.maximum(slack, 0))
    passed = jax.random.randint(jax.random.fold_in(own, 4), (count // 2,), 0, 1 << 20) % (slack + 1)
    sizes = sizes.at[source_of].add(-passed).at[taker].add(passed)
    labels = jnp.searchsorted(jnp.cumsum(sizes), jnp.arange(rows * top), side="right").astype(jnp.int32)
    grid = labels.reshape(top, rows).T
    grid = grid[jax.random.permutation(jax.random.fold_in(own, 1), rows)]
    turn = jax.random.randint(jax.random.fold_in(own, 2), (rows, 1), 0, top)
    return jnp.take_along_axis(grid, (jnp.arange(top)[None, :] + turn) % top, axis=1)


def shares(number_of, total, reach, skew, full):
    portions = [(1 << 20) // math.isqrt(grade ** skew) + 1 for grade in range(1, number_of + 1)]
    largest = reach if full else min(reach, max(-(-total // number_of), total * portions[0] // sum(portions)))
    least = 1 if total - largest >= number_of - 1 else 0
    holding, spare = [largest] + [least] * (number_of - 1), total - largest - least * (number_of - 1)
    while spare > 0:
        candidates = [i for i in range(1, number_of) if holding[i] < largest] or [i for i in range(1, number_of) if holding[i] < reach]
        whole, left = sum([portions[i] for i in candidates]), spare
        for i in candidates:
            addition = min(reach - holding[i], max(1, left * portions[i] // whole), spare)
            holding[i] = holding[i] + addition
            spare = spare - addition
    return np.array(holding)


def noise(own_key, shape, deviation, limit, cuts=(), kind=jnp.bfloat16):
    factor_of = block_scale(own_key, shape, cuts, -0.22, 0.18) if cuts else 1.0
    values = jax.random.normal(own_key, shape, jnp.float32) * deviation * factor_of
    return jnp.minimum(jnp.maximum(values, -limit), limit).astype(kind)


def noise_with(stream_key, dims, spread, reach, cuts, heavy, kind=jnp.bfloat16):
    values = spread * jax.random.normal(stream_key, dims, jnp.float32)
    if cuts:
        values = values * block_scale(stream_key, dims, cuts, -0.22, 0.18)
    return jnp.clip(raised(values, jax.random.fold_in(stream_key, 3), *heavy), -reach, reach).astype(kind)


def setup_inputs(seed: int = 0) -> dict:
    key_of = jax.random.split(jax.random.key(seed), 8)
    queries = draw_queries(jax.random.fold_in(key_of[7], 71), 0)
    keys = noise(key_of[1], (TOKENS, HEADS, HD), 1.0, 6.0, ((0, 64), (1, 8)))
    values = noise(key_of[2], (TOKENS, HEADS, HD), 1.0, 6.0, ((0, 64), (1, 8)))
    clusters_keys = jax.random.split(jax.random.fold_in(key_of[3], 1), HEADS * TOKENS // TOK_DEV)
    clusters_turns = jax.random.permutation(jax.random.fold_in(key_of[3], 3), HEADS * TOKENS // TOK_DEV)
    clusters = jax.vmap(lambda own, number: deal_out(jax.random.fold_in(key_of[3], 2), own, number, TOK_DEV, CLUSTERS, 1, MOST, 2))(clusters_keys, clusters_turns).reshape((HEADS, TOKENS, 1))
    cent_keys = draw_cent_keys(jax.random.fold_in(key_of[7], 71), 0)
    cent_values = noise(key_of[5], (HEADS, CLUSTERS, HD), 1.0, 6.0, ((0, 8), (1, 64)))
    out_weight = noise_with(key_of[6], (HEADS * HD, D), (HEADS * HD) ** -0.5, 0.1875, ((0, 8),), (0, 1, 8, 2.0))
    return {"queries": queries, "keys": keys, "values": values, "clusters": clusters, "cent_keys": cent_keys, "cent_values": cent_values, "out_weight": out_weight}


def one_head(queries_h, keys_h, values_h, assign, cent_k, cent_v):
    tokens = queries_h.shape[0]
    capacity = N_SEQ * MOST
    scale = HD ** -0.5
    order = jnp.arange(tokens, dtype=jnp.int32)
    sort_idx = jnp.argsort(assign, stable=True).astype(jnp.int32)
    sorted_c = assign[sort_idx].astype(jnp.int32)
    first = jnp.searchsorted(sorted_c, sorted_c, side="left").astype(jnp.int32)
    rank = order - first
    table = jnp.full((CLUSTERS, capacity), tokens, jnp.int32).at[sorted_c, rank].set(sort_idx)
    zero_row = jnp.zeros((1, HD), jnp.bfloat16)
    q_pad = jnp.concatenate([queries_h, zero_row], axis=0)
    k_pad = jnp.concatenate([keys_h, zero_row], axis=0)
    v_pad = jnp.concatenate([values_h, zero_row], axis=0)
    p_pad = jnp.concatenate([order, jnp.full((1,), -1, jnp.int32)], axis=0)
    q_grp = q_pad[table].astype(jnp.float32)
    k_grp = k_pad[table].astype(jnp.float32)
    v_grp = v_pad[table].astype(jnp.float32)
    p_grp = p_pad[table]
    local = jnp.einsum("cie,cje->cij", q_grp, k_grp) * scale
    allowed = (p_grp[:, None, :] >= 0) & (p_grp[:, None, :] <= p_grp[:, :, None])
    local = jnp.where(allowed, local, -1e30)
    memory = jnp.einsum("cie,de->cid", q_grp, cent_k.astype(jnp.float32)) * scale
    scores = jnp.concatenate([local, memory], axis=-1)
    top = jnp.max(scores, axis=-1, keepdims=True)
    weight = jnp.exp(scores - top)
    rounded = lax.optimization_barrier(weight.astype(jnp.bfloat16)).astype(jnp.float32)
    numer = jnp.einsum("cij,cje->cie", rounded[..., :capacity], v_grp)
    numer = numer + jnp.einsum("cid,de->cie", rounded[..., capacity:], cent_v.astype(jnp.float32))
    result = (numer / jnp.sum(weight, axis=-1, keepdims=True)).astype(jnp.bfloat16)
    placed = jnp.zeros((tokens + 1, HD), jnp.bfloat16).at[table].set(result)
    return placed[:tokens]


def reference(queries, keys, values, clusters, cent_keys, cent_values, out_weight):
    tokens = queries.shape[0]

    def per_head(items):
        return one_head(items[0], items[1], items[2], items[3], items[4], items[5])

    attended = lax.map(per_head, (jnp.swapaxes(queries, 0, 1), jnp.swapaxes(keys, 0, 1), jnp.swapaxes(values, 0, 1), clusters[:, :, 0], cent_keys, cent_values))
    flat = jnp.swapaxes(attended, 0, 1).reshape(tokens, HEADS * HD)
    group = (HEADS // N_HEAD) * HD

    def add_group(index, total):
        start = index * group
        cols = lax.dynamic_slice_in_dim(flat, start, group, 1)
        rows = lax.dynamic_slice_in_dim(out_weight, start, group, 0)
        partial_sum = jnp.dot(cols, rows, preferred_element_type=jnp.float32)
        return total + lax.optimization_barrier(partial_sum.astype(jnp.bfloat16)).astype(jnp.float32)

    total = lax.fori_loop(0, N_HEAD, add_group, jnp.zeros((tokens, D), jnp.float32))
    return total.T.astype(jnp.bfloat16)
```

```python
import jax
import jax.numpy as jnp
from jax import lax
from jax.sharding import PartitionSpec as P

CLUSTERS = 256
MOST = 8


def on_device(queries, keys, values, clusters, cent_keys, cent_values, out_weight):
    tok_dev, heads_dev, head_dim = queries.shape
    owners = lax.axis_size("seq")
    per_owner = CLUSTERS // owners
    group = per_owner * MOST
    width = heads_dev * head_dim
    cent_rows = 2 * per_owner
    count_rows = 8
    scale = head_dim ** (-0.5)
    dtype = queries.dtype

    assign = clusters[:, :, 0]
    order = jnp.arange(tok_dev, dtype=jnp.int32)
    earlier = (assign[:, :, None] == assign[:, None, :]) & (
        order[None, None, :] < order[None, :, None]
    )
    rank = jnp.sum(earlier.astype(jnp.int32), axis=2)
    slot_of = (assign * MOST + rank).T
    head_cols = jnp.arange(heads_dev, dtype=jnp.int32)[None, :]
    owner_of = slot_of // group
    within = slot_of % group

    counts = jnp.sum(
        (assign[:, :, None] == jnp.arange(CLUSTERS, dtype=jnp.int32)[None, None, :]).astype(jnp.int32),
        axis=1,
    )
    counts = jnp.transpose(counts.reshape(heads_dev, owners, per_owner), (1, 0, 2))
    counts = counts.reshape(owners, heads_dev * per_owner).astype(dtype)
    counts = jnp.pad(counts, ((0, 0), (0, count_rows * width - heads_dev * per_owner)))
    counts = counts.reshape(owners, count_rows, width)

    rows = jnp.stack([queries, keys, values], axis=2)
    body = jnp.zeros((owners, 3, group, heads_dev, head_dim), dtype)
    body = body.at[owner_of, :, within, head_cols].set(rows)
    body = body.reshape(owners, 3 * group, width)
    cent = jnp.stack([cent_keys, cent_values], axis=0).reshape(1, cent_rows, width)
    cent = jnp.broadcast_to(cent, (owners, cent_rows, width))
    send = jnp.concatenate([body, cent, counts], axis=1)
    recv = lax.all_to_all(send, "seq", split_axis=0, concat_axis=0, tiled=True)

    five = (owners, per_owner, MOST, heads_dev, head_dim)
    q_in = recv[:, 0:group].reshape(five)
    k_in = recv[:, group : 2 * group].reshape(five)
    v_in = recv[:, 2 * group : 3 * group].reshape(five)
    cent_in = recv[:, 3 * group : 3 * group + cent_rows].reshape(
        owners, 2, heads_dev, per_owner, head_dim
    )
    cent_in = jnp.transpose(cent_in, (1, 2, 0, 3, 4)).reshape(2, heads_dev, CLUSTERS, head_dim)
    cent_k_all, cent_v_all = cent_in[0], cent_in[1]
    cnt = recv[:, 3 * group + cent_rows, : heads_dev * per_owner].astype(jnp.int32)
    cnt = cnt.reshape(owners, heads_dev, per_owner)

    span = owners * MOST
    local = jnp.einsum("acrhe,bcshe->charbs", q_in, k_in, preferred_element_type=jnp.float32)
    local = local.reshape(per_owner, heads_dev, span, span) * scale
    depth = jnp.arange(MOST, dtype=jnp.int32)
    valid = depth[None, None, None, :] < jnp.transpose(cnt, (2, 1, 0))[..., None]
    valid = valid.reshape(per_owner, heads_dev, span)
    line = jnp.arange(span, dtype=jnp.int32)
    allowed = valid[:, :, None, :] & (line[None, :] <= line[:, None])[None, None]
    local = jnp.where(allowed, local, -1e30)
    memory = jnp.einsum("acrhe,hde->chard", q_in, cent_k_all, preferred_element_type=jnp.float32)
    memory = memory.reshape(per_owner, heads_dev, span, CLUSTERS) * scale
    top = jnp.maximum(jnp.max(local, axis=-1), jnp.max(memory, axis=-1))[..., None]
    w_local = jnp.exp(local - top)
    w_memory = jnp.exp(memory - top)
    denom = jnp.sum(w_local, axis=-1) + jnp.sum(w_memory, axis=-1)
    numer = jnp.einsum(
        "chrbs,bcshe->chre",
        w_local.astype(dtype).reshape(per_owner, heads_dev, span, owners, MOST),
        v_in,
        preferred_element_type=jnp.float32,
    )
    numer = numer + jnp.einsum(
        "chrd,hde->chre", w_memory.astype(dtype), cent_v_all, preferred_element_type=jnp.float32
    )
    result = (numer / denom[..., None]).astype(dtype)
    result = result.reshape(per_owner, heads_dev, owners, MOST, head_dim)
    back = jnp.transpose(result, (2, 0, 3, 1, 4)).reshape(owners, group, width)
    back = lax.all_to_all(back, "seq", split_axis=0, concat_axis=0, tiled=True)
    back = back.reshape(owners * group, heads_dev, head_dim)
    attended = back[slot_of, head_cols]

    flat_out = attended.reshape(tok_dev, heads_dev * head_dim)
    return lax.psum_scatter(
        jnp.einsum("kc,tk->ct", out_weight, flat_out, preferred_element_type=jnp.float32).astype(
            jnp.bfloat16
        ),
        "head",
        scatter_dimension=0,
        tiled=True,
    )


def solution(mesh):
    return jax.shard_map(
        on_device,
        mesh=mesh,
        in_specs=(
            P("seq", "head", None),
            P("seq", "head", None),
            P("seq", "head", None),
            P("head", "seq", None),
            P("head", "seq", None),
            P("head", "seq", None),
            P("head", None),
        ),
        out_specs=P("head", "seq"),
        check_vma=False,
    )
```

```python
import jax
import jax.numpy as jnp
from jax import lax
from jax.sharding import PartitionSpec as P

CLUSTERS = 256
MOST = 8


def on_device(queries, keys, values, clusters, cent_keys, cent_values, out_weight):
    tok_dev, heads_dev, head_dim = queries.shape
    owners = lax.axis_size("seq")
    per_owner = CLUSTERS // owners
    group = per_owner * MOST
    width = heads_dev * head_dim
    cent_rows = 2 * per_owner
    count_rows = 8
    scale = head_dim ** (-0.5)
    dtype = queries.dtype

    assign = clusters[:, :, 0]
    order = jnp.arange(tok_dev, dtype=jnp.int32)
    earlier = (assign[:, :, None] == assign[:, None, :]) & (
        order[None, None, :] < order[None, :, None]
    )
    rank = jnp.sum(earlier.astype(jnp.int32), axis=2)
    slot_of = (assign * MOST + rank).T
    head_cols = jnp.arange(heads_dev, dtype=jnp.int32)[None, :]

    counts = jnp.sum(
        (assign[:, :, None] == jnp.arange(CLUSTERS, dtype=jnp.int32)[None, None, :]).astype(jnp.int32),
        axis=1,
    )
    counts = jnp.transpose(counts.reshape(heads_dev, owners, per_owner), (1, 0, 2))
    counts = counts.reshape(owners, heads_dev * per_owner).astype(dtype)
    counts = jnp.pad(counts, ((0, 0), (0, count_rows * width - heads_dev * per_owner)))
    counts = counts.reshape(owners, count_rows, width)

    slot_ids = jnp.arange(owners * group, dtype=jnp.int32)
    onehot = (slot_of.T[:, None, :] == slot_ids[None, :, None]).astype(dtype)
    onehot = onehot.reshape(heads_dev, owners, group, tok_dev)
    rows = jnp.stack([queries, keys, values], axis=1)
    body = jnp.einsum("hogt,tkhe->okghe", onehot, rows, preferred_element_type=jnp.float32)
    body = body.astype(dtype).reshape(owners, 3 * group, width)
    cent = jnp.stack([cent_keys, cent_values], axis=0).reshape(1, cent_rows, width)
    cent = jnp.broadcast_to(cent, (owners, cent_rows, width))
    send = jnp.concatenate([body, cent, counts], axis=1)
    recv = lax.all_to_all(send, "seq", split_axis=0, concat_axis=0, tiled=True)

    five = (owners, per_owner, MOST, heads_dev, head_dim)
    q_in = recv[:, 0:group].reshape(five)
    k_in = recv[:, group : 2 * group].reshape(five)
    v_in = recv[:, 2 * group : 3 * group].reshape(five)
    cent_in = recv[:, 3 * group : 3 * group + cent_rows].reshape(
        owners, 2, heads_dev, per_owner, head_dim
    )
    cent_in = jnp.transpose(cent_in, (1, 2, 0, 3, 4)).reshape(2, heads_dev, CLUSTERS, head_dim)
    cent_k_all, cent_v_all = cent_in[0], cent_in[1]
    cnt = recv[:, 3 * group + cent_rows, : heads_dev * per_owner].astype(jnp.int32)
    cnt = cnt.reshape(owners, heads_dev, per_owner)

    span = owners * MOST
    local = jnp.einsum("acrhe,bcshe->charbs", q_in, k_in, preferred_element_type=jnp.float32)
    local = local.reshape(per_owner, heads_dev, span, span) * scale
    depth = jnp.arange(MOST, dtype=jnp.int32)
    valid = depth[None, None, None, :] < jnp.transpose(cnt, (2, 1, 0))[..., None]
    valid = valid.reshape(per_owner, heads_dev, span)
    line = jnp.arange(span, dtype=jnp.int32)
    allowed = valid[:, :, None, :] & (line[None, :] <= line[:, None])[None, None]
    local = jnp.where(allowed, local, -1e30)
    memory = jnp.einsum("acrhe,hde->chard", q_in, cent_k_all, preferred_element_type=jnp.float32)
    memory = memory.reshape(per_owner, heads_dev, span, CLUSTERS) * scale
    top = jnp.maximum(jnp.max(local, axis=-1), jnp.max(memory, axis=-1))[..., None]
    w_local = jnp.exp(local - top)
    w_memory = jnp.exp(memory - top)
    denom = jnp.sum(w_local, axis=-1) + jnp.sum(w_memory, axis=-1)
    numer = jnp.einsum(
        "chrbs,bcshe->chre",
        w_local.astype(dtype).reshape(per_owner, heads_dev, span, owners, MOST),
        v_in,
        preferred_element_type=jnp.float32,
    )
    numer = numer + jnp.einsum(
        "chrd,hde->chre", w_memory.astype(dtype), cent_v_all, preferred_element_type=jnp.float32
    )
    result = (numer / denom[..., None]).astype(dtype)
    result = result.reshape(per_owner, heads_dev, owners, MOST, head_dim)
    back = jnp.transpose(result, (2, 0, 3, 1, 4)).reshape(owners, group, width)
    back = lax.all_to_all(back, "seq", split_axis=0, concat_axis=0, tiled=True)
    back = back.reshape(owners * group, heads_dev, head_dim)
    attended = back[slot_of, head_cols]

    flat_out = attended.reshape(tok_dev, heads_dev * head_dim)
    return lax.psum_scatter(
        jnp.einsum("kc,tk->ct", out_weight, flat_out, preferred_element_type=jnp.float32).astype(
            jnp.bfloat16
        ),
        "head",
        scatter_dimension=0,
        tiled=True,
    )


def solution(mesh):
    return jax.shard_map(
        on_device,
        mesh=mesh,
        in_specs=(
            P("seq", "head", None),
            P("seq", "head", None),
            P("seq", "head", None),
            P("head", "seq", None),
            P("head", "seq", None),
            P("head", "seq", None),
            P("head", None),
        ),
        out_specs=P("head", "seq"),
        check_vma=False,
    )
```

```python
import functools

import jax
import jax.numpy as jnp
from jax import lax
from jax.experimental import pallas as pl
from jax.sharding import PartitionSpec as P

CLUSTERS = 256
MOST = 8


def attention_kernel(q_ref, k_ref, v_ref, ck_ref, cv_ref, valid_ref, out_ref, *, scale):
    q = q_ref[0, 0, 0]
    k = k_ref[0, 0, 0]
    v = v_ref[0, 0, 0]
    ck = ck_ref[0, 0]
    cv = cv_ref[0, 0]
    span = q.shape[0]
    contract = (((1,), (1,)), ((), ()))
    local = lax.dot_general(q, k, contract, preferred_element_type=jnp.float32) * scale
    row = lax.broadcasted_iota(jnp.int32, (span, span), 0)
    col = lax.broadcasted_iota(jnp.int32, (span, span), 1)
    allowed = (col <= row) & (valid_ref[0, 0] > 0.5)
    local = jnp.where(allowed, local, -1e30)
    memory = lax.dot_general(q, ck, contract, preferred_element_type=jnp.float32) * scale
    top = jnp.maximum(
        jnp.max(local, axis=1, keepdims=True), jnp.max(memory, axis=1, keepdims=True)
    )
    w_local = jnp.exp(local - top)
    w_memory = jnp.exp(memory - top)
    denom = jnp.sum(w_local, axis=1, keepdims=True) + jnp.sum(w_memory, axis=1, keepdims=True)
    numer = jnp.dot(w_local.astype(v.dtype), v, preferred_element_type=jnp.float32)
    numer = numer + jnp.dot(w_memory.astype(cv.dtype), cv, preferred_element_type=jnp.float32)
    out_ref[0, 0] = (numer / denom).astype(out_ref.dtype)


def cluster_attention(qkv, cent, valid, scale):
    _, per_owner, heads_dev, span, head_dim = qkv.shape
    clusters = cent.shape[2]

    def pick(kind):
        return pl.BlockSpec((1, 1, 1, span, head_dim), lambda c, h: (kind, c, h, 0, 0))

    def centroid(kind):
        return pl.BlockSpec((1, 1, clusters, head_dim), lambda c, h: (kind, h, 0, 0))

    return pl.pallas_call(
        functools.partial(attention_kernel, scale=scale),
        grid=(per_owner, heads_dev),
        in_specs=[
            pick(0),
            pick(1),
            pick(2),
            centroid(0),
            centroid(1),
            pl.BlockSpec((1, 1, 1, span), lambda c, h: (c, h, 0, 0)),
        ],
        out_specs=pl.BlockSpec((1, 1, span, head_dim), lambda c, h: (c, h, 0, 0)),
        out_shape=jax.ShapeDtypeStruct((per_owner, heads_dev, span, head_dim), qkv.dtype),
    )(qkv, qkv, qkv, cent, cent, valid)


def on_device(queries, keys, values, clusters, cent_keys, cent_values, out_weight):
    tok_dev, heads_dev, head_dim = queries.shape
    owners = lax.axis_size("seq")
    per_owner = CLUSTERS // owners
    group = per_owner * MOST
    width = heads_dev * head_dim
    cent_rows = 2 * per_owner
    count_rows = 8
    scale = head_dim ** (-0.5)
    dtype = queries.dtype

    assign = clusters[:, :, 0]
    order = jnp.arange(tok_dev, dtype=jnp.int32)
    earlier = (assign[:, :, None] == assign[:, None, :]) & (
        order[None, None, :] < order[None, :, None]
    )
    rank = jnp.sum(earlier.astype(jnp.int32), axis=2)
    slot_of = (assign * MOST + rank).T
    head_cols = jnp.arange(heads_dev, dtype=jnp.int32)[None, :]

    counts = jnp.sum(
        (assign[:, :, None] == jnp.arange(CLUSTERS, dtype=jnp.int32)[None, None, :]).astype(jnp.int32),
        axis=1,
    )
    counts = jnp.transpose(counts.reshape(heads_dev, owners, per_owner), (1, 0, 2))
    counts = counts.reshape(owners, heads_dev * per_owner).astype(dtype)
    counts = jnp.pad(counts, ((0, 0), (0, count_rows * width - heads_dev * per_owner)))
    counts = counts.reshape(owners, count_rows, width)

    slot_ids = jnp.arange(owners * group, dtype=jnp.int32)
    onehot = (slot_of.T[:, None, :] == slot_ids[None, :, None]).astype(dtype)
    onehot = onehot.reshape(heads_dev, owners, group, tok_dev)
    rows = jnp.stack([queries, keys, values], axis=1)
    body = jnp.einsum("hogt,tkhe->okghe", onehot, rows, preferred_element_type=jnp.float32)
    body = body.astype(dtype).reshape(owners, 3 * group, width)
    cent = jnp.stack([cent_keys, cent_values], axis=0).reshape(1, cent_rows, width)
    cent = jnp.broadcast_to(cent, (owners, cent_rows, width))
    send = jnp.concatenate([body, cent, counts], axis=1)
    recv = lax.all_to_all(send, "seq", split_axis=0, concat_axis=0, tiled=True)

    span = owners * MOST
    qkv = recv[:, 0 : 3 * group].reshape(owners, 3, per_owner, MOST, heads_dev, head_dim)
    qkv = jnp.transpose(qkv, (1, 2, 4, 0, 3, 5)).reshape(3, per_owner, heads_dev, span, head_dim)
    cent_in = recv[:, 3 * group : 3 * group + cent_rows].reshape(
        owners, 2, heads_dev, per_owner, head_dim
    )
    cent_in = jnp.transpose(cent_in, (1, 2, 0, 3, 4)).reshape(2, heads_dev, CLUSTERS, head_dim)
    cnt = recv[:, 3 * group + cent_rows, : heads_dev * per_owner].astype(jnp.int32)
    cnt = cnt.reshape(owners, heads_dev, per_owner)
    depth = jnp.arange(MOST, dtype=jnp.int32)
    valid = depth[None, None, None, :] < jnp.transpose(cnt, (2, 1, 0))[..., None]
    valid = valid.astype(jnp.float32).reshape(per_owner, heads_dev, 1, span)

    result = cluster_attention(qkv, cent_in, valid, scale)
    result = result.reshape(per_owner, heads_dev, owners, MOST, head_dim)
    back = jnp.transpose(result, (2, 0, 3, 1, 4)).reshape(owners, group, width)
    back = lax.all_to_all(back, "seq", split_axis=0, concat_axis=0, tiled=True)
    back = back.reshape(owners * group, heads_dev, head_dim)
    attended = back[slot_of, head_cols]

    flat_out = attended.reshape(tok_dev, heads_dev * head_dim)
    return lax.psum_scatter(
        jnp.einsum("kc,tk->ct", out_weight, flat_out, preferred_element_type=jnp.float32).astype(
            jnp.bfloat16
        ),
        "head",
        scatter_dimension=0,
        tiled=True,
    )


def solution(mesh):
    return jax.shard_map(
        on_device,
        mesh=mesh,
        in_specs=(
            P("seq", "head", None),
            P("seq", "head", None),
            P("seq", "head", None),
            P("head", "seq", None),
            P("head", "seq", None),
            P("head", "seq", None),
            P("head", None),
        ),
        out_specs=P("head", "seq"),
        check_vma=False,
    )
```

```python
import functools

import jax
import jax.numpy as jnp
from jax import lax
from jax.experimental import pallas as pl
from jax.sharding import PartitionSpec as P

CLUSTERS = 256
MOST = 8


def attention_kernel(q_ref, k_ref, v_ref, ck_ref, cv_ref, valid_ref, out_ref, *, scale):
    q = q_ref[0, 0, 0]
    k = k_ref[0, 0, 0]
    v = v_ref[0, 0, 0]
    ck = ck_ref[0, 0]
    cv = cv_ref[0, 0]
    span = q.shape[0]
    contract = (((1,), (1,)), ((), ()))
    local = lax.dot_general(q, k, contract, preferred_element_type=jnp.float32) * scale
    row = lax.broadcasted_iota(jnp.int32, (span, span), 0)
    col = lax.broadcasted_iota(jnp.int32, (span, span), 1)
    allowed = (col <= row) & (valid_ref[0, 0] > 0.5)
    local = jnp.where(allowed, local, -1e30)
    memory = lax.dot_general(q, ck, contract, preferred_element_type=jnp.float32) * scale
    top = jnp.maximum(
        jnp.max(local, axis=1, keepdims=True), jnp.max(memory, axis=1, keepdims=True)
    )
    w_local = jnp.exp(local - top)
    w_memory = jnp.exp(memory - top)
    denom = jnp.sum(w_local, axis=1, keepdims=True) + jnp.sum(w_memory, axis=1, keepdims=True)
    numer = jnp.dot(w_local.astype(v.dtype), v, preferred_element_type=jnp.float32)
    numer = numer + jnp.dot(w_memory.astype(cv.dtype), cv, preferred_element_type=jnp.float32)
    out_ref[0, 0] = (numer / denom).astype(out_ref.dtype)


def cluster_attention(qkv, cent, valid, scale):
    _, per_owner, heads_dev, span, head_dim = qkv.shape
    clusters = cent.shape[2]

    def pick(kind):
        return pl.BlockSpec((1, 1, 1, span, head_dim), lambda c, h: (kind, c, h, 0, 0))

    def centroid(kind):
        return pl.BlockSpec((1, 1, clusters, head_dim), lambda c, h: (kind, h, 0, 0))

    return pl.pallas_call(
        functools.partial(attention_kernel, scale=scale),
        grid=(per_owner, heads_dev),
        in_specs=[
            pick(0),
            pick(1),
            pick(2),
            centroid(0),
            centroid(1),
            pl.BlockSpec((1, 1, 1, span), lambda c, h: (c, h, 0, 0)),
        ],
        out_specs=pl.BlockSpec((1, 1, span, head_dim), lambda c, h: (c, h, 0, 0)),
        out_shape=jax.ShapeDtypeStruct((per_owner, heads_dev, span, head_dim), qkv.dtype),
    )(qkv, qkv, qkv, cent, cent, valid)


def on_device(queries, keys, values, clusters, cent_keys, cent_values, out_weight):
    tok_dev, heads_dev, head_dim = queries.shape
    owners = lax.axis_size("seq")
    per_owner = CLUSTERS // owners
    group = per_owner * MOST
    width = heads_dev * head_dim
    cent_rows = 2 * per_owner
    count_rows = 8
    scale = head_dim ** (-0.5)
    dtype = queries.dtype

    n_head = lax.axis_size("head")
    rows_dev, features = out_weight.shape
    feat = features // n_head
    w_parts = jnp.transpose(out_weight.reshape(rows_dev, n_head, feat), (1, 0, 2))
    w_mine = lax.all_to_all(w_parts, "head", split_axis=0, concat_axis=0, tiled=True)

    assign = clusters[:, :, 0]
    order = jnp.arange(tok_dev, dtype=jnp.int32)
    earlier = (assign[:, :, None] == assign[:, None, :]) & (
        order[None, None, :] < order[None, :, None]
    )
    rank = jnp.sum(earlier.astype(jnp.int32), axis=2)
    slot_of = (assign * MOST + rank).T
    head_cols = jnp.arange(heads_dev, dtype=jnp.int32)[None, :]

    counts = jnp.sum(
        (assign[:, :, None] == jnp.arange(CLUSTERS, dtype=jnp.int32)[None, None, :]).astype(jnp.int32),
        axis=1,
    )
    counts = jnp.transpose(counts.reshape(heads_dev, owners, per_owner), (1, 0, 2))
    counts = counts.reshape(owners, heads_dev * per_owner).astype(dtype)
    counts = jnp.pad(counts, ((0, 0), (0, count_rows * width - heads_dev * per_owner)))
    counts = counts.reshape(owners, count_rows, width)

    slot_ids = jnp.arange(owners * group, dtype=jnp.int32)
    onehot = (slot_of.T[:, None, :] == slot_ids[None, :, None]).astype(dtype)
    onehot = onehot.reshape(heads_dev, owners, group, tok_dev)
    rows = jnp.stack([queries, keys, values], axis=1)
    body = jnp.einsum("hogt,tkhe->okghe", onehot, rows, preferred_element_type=jnp.float32)
    body = body.astype(dtype).reshape(owners, 3 * group, width)
    cent = jnp.stack([cent_keys, cent_values], axis=0).reshape(1, cent_rows, width)
    cent = jnp.broadcast_to(cent, (owners, cent_rows, width))
    send = jnp.concatenate([body, cent, counts], axis=1)
    recv = lax.all_to_all(send, "seq", split_axis=0, concat_axis=0, tiled=True)
    recv, w_mine = lax.optimization_barrier((recv, w_mine))

    span = owners * MOST
    qkv = recv[:, 0 : 3 * group].reshape(owners, 3, per_owner, MOST, heads_dev, head_dim)
    qkv = jnp.transpose(qkv, (1, 2, 4, 0, 3, 5)).reshape(3, per_owner, heads_dev, span, head_dim)
    cent_in = recv[:, 3 * group : 3 * group + cent_rows].reshape(
        owners, 2, heads_dev, per_owner, head_dim
    )
    cent_in = jnp.transpose(cent_in, (1, 2, 0, 3, 4)).reshape(2, heads_dev, CLUSTERS, head_dim)
    cnt = recv[:, 3 * group + cent_rows, : heads_dev * per_owner].astype(jnp.int32)
    cnt = cnt.reshape(owners, heads_dev, per_owner)
    depth = jnp.arange(MOST, dtype=jnp.int32)
    valid = depth[None, None, None, :] < jnp.transpose(cnt, (2, 1, 0))[..., None]
    valid = valid.astype(jnp.float32).reshape(per_owner, heads_dev, 1, span)

    result = cluster_attention(qkv, cent_in, valid, scale)
    result = result.reshape(per_owner, heads_dev, owners, MOST, head_dim)
    back = jnp.transpose(result, (2, 0, 3, 1, 4)).reshape(owners, group, width)
    back = lax.all_to_all(back, "seq", split_axis=0, concat_axis=0, tiled=True)
    back = back.reshape(owners * group, heads_dev, head_dim)
    attended = back[slot_of, head_cols]

    flat_out = attended.reshape(tok_dev, heads_dev * head_dim)
    att_all = lax.all_gather(flat_out, "head", axis=0, tiled=False)
    partial = jnp.einsum("gkf,gtk->gft", w_mine, att_all, preferred_element_type=jnp.float32)
    total = jnp.sum(partial.astype(jnp.bfloat16).astype(jnp.float32), axis=0)
    return total.astype(jnp.bfloat16)


def solution(mesh):
    return jax.shard_map(
        on_device,
        mesh=mesh,
        in_specs=(
            P("seq", "head", None),
            P("seq", "head", None),
            P("seq", "head", None),
            P("head", "seq", None),
            P("head", "seq", None),
            P("head", "seq", None),
            P("head", None),
        ),
        out_specs=P("head", "seq"),
        check_vma=False,
    )
```

```python
import functools

import jax
import jax.numpy as jnp
from jax import lax
from jax.experimental import pallas as pl
from jax.sharding import PartitionSpec as P

CLUSTERS = 256
MOST = 8


def attention_kernel(q_ref, k_ref, v_ref, ck_ref, cv_ref, valid_ref, out_ref, *, scale):
    sources, depth, head_dim = q_ref.shape
    span = sources * depth

    def flat(ref):
        return ref[...].astype(jnp.float32).reshape(span, head_dim).astype(ref.dtype)

    q = flat(q_ref)
    k = flat(k_ref)
    v = flat(v_ref)
    ck = ck_ref[0, 0]
    cv = cv_ref[0, 0]
    contract = (((1,), (1,)), ((), ()))
    local = lax.dot_general(q, k, contract, preferred_element_type=jnp.float32) * scale
    row = lax.broadcasted_iota(jnp.int32, (span, span), 0)
    col = lax.broadcasted_iota(jnp.int32, (span, span), 1)
    allowed = (col <= row) & (valid_ref[0, 0] > 0.5)
    local = jnp.where(allowed, local, -1e30)
    memory = lax.dot_general(q, ck, contract, preferred_element_type=jnp.float32) * scale
    top = jnp.maximum(
        jnp.max(local, axis=1, keepdims=True), jnp.max(memory, axis=1, keepdims=True)
    )
    w_local = jnp.exp(local - top)
    w_memory = jnp.exp(memory - top)
    denom = jnp.sum(w_local, axis=1, keepdims=True) + jnp.sum(w_memory, axis=1, keepdims=True)
    numer = jnp.dot(w_local.astype(v.dtype), v, preferred_element_type=jnp.float32)
    numer = numer + jnp.dot(w_memory.astype(cv.dtype), cv, preferred_element_type=jnp.float32)
    result = (numer / denom).astype(out_ref.dtype).astype(jnp.float32)
    out_ref[...] = result.reshape(sources, depth, head_dim).astype(out_ref.dtype)


def cluster_attention(recv, cent, valid, scale, per_owner, heads_dev):
    sources, _, width = recv.shape
    head_dim = width // heads_dev
    clusters = cent.shape[2]

    def pick(kind):
        return pl.BlockSpec(
            (sources, MOST, head_dim), lambda c, h: (0, kind * per_owner + c, h)
        )

    def centroid(kind):
        return pl.BlockSpec((1, 1, clusters, head_dim), lambda c, h: (kind, h, 0, 0))

    return pl.pallas_call(
        functools.partial(attention_kernel, scale=scale),
        grid=(per_owner, heads_dev),
        in_specs=[
            pick(0),
            pick(1),
            pick(2),
            centroid(0),
            centroid(1),
            pl.BlockSpec((1, 1, 1, sources * MOST), lambda c, h: (c, h, 0, 0)),
        ],
        out_specs=pl.BlockSpec((sources, MOST, head_dim), lambda c, h: (0, c, h)),
        out_shape=jax.ShapeDtypeStruct((sources, per_owner * MOST, width), recv.dtype),
    )(recv, recv, recv, cent, cent, valid)


def on_device(queries, keys, values, clusters, cent_keys, cent_values, out_weight):
    tok_dev, heads_dev, head_dim = queries.shape
    owners = lax.axis_size("seq")
    per_owner = CLUSTERS // owners
    group = per_owner * MOST
    width = heads_dev * head_dim
    cent_rows = 2 * per_owner
    count_rows = 8
    scale = head_dim ** (-0.5)
    dtype = queries.dtype

    assign = clusters[:, :, 0]
    order = jnp.arange(tok_dev, dtype=jnp.int32)
    earlier = (assign[:, :, None] == assign[:, None, :]) & (
        order[None, None, :] < order[None, :, None]
    )
    rank = jnp.sum(earlier.astype(jnp.int32), axis=2)
    slot_of = (assign * MOST + rank).T
    head_cols = jnp.arange(heads_dev, dtype=jnp.int32)[None, :]

    counts = jnp.sum(
        (assign[:, :, None] == jnp.arange(CLUSTERS, dtype=jnp.int32)[None, None, :]).astype(jnp.int32),
        axis=1,
    )
    counts = jnp.transpose(counts.reshape(heads_dev, owners, per_owner), (1, 0, 2))
    counts = counts.reshape(owners, heads_dev * per_owner).astype(dtype)
    counts = jnp.pad(counts, ((0, 0), (0, count_rows * width - heads_dev * per_owner)))
    counts = counts.reshape(owners, count_rows, width)

    slot_ids = jnp.arange(owners * group, dtype=jnp.int32)
    onehot = (slot_of.T[:, None, :] == slot_ids[None, :, None]).astype(dtype)
    onehot = onehot.reshape(heads_dev, owners, group, tok_dev)
    rows = jnp.stack([queries, keys, values], axis=1)
    body = jnp.einsum("hogt,tkhe->okghe", onehot, rows, preferred_element_type=jnp.float32)
    body = body.astype(dtype).reshape(owners, 3 * group, width)
    cent = jnp.stack([cent_keys, cent_values], axis=0).reshape(1, cent_rows, width)
    cent = jnp.broadcast_to(cent, (owners, cent_rows, width))
    send = jnp.concatenate([body, cent, counts], axis=1)
    recv = lax.all_to_all(send, "seq", split_axis=0, concat_axis=0, tiled=True)

    span = owners * MOST
    cent_in = recv[:, 3 * group : 3 * group + cent_rows].reshape(
        owners, 2, heads_dev, per_owner, head_dim
    )
    cent_in = jnp.transpose(cent_in, (1, 2, 0, 3, 4)).reshape(2, heads_dev, CLUSTERS, head_dim)
    cnt = recv[:, 3 * group + cent_rows, : heads_dev * per_owner].astype(jnp.int32)
    cnt = cnt.reshape(owners, heads_dev, per_owner)
    depth = jnp.arange(MOST, dtype=jnp.int32)
    valid = depth[None, None, None, :] < jnp.transpose(cnt, (2, 1, 0))[..., None]
    valid = valid.astype(jnp.float32).reshape(per_owner, heads_dev, 1, span)

    back = cluster_attention(recv, cent_in, valid, scale, per_owner, heads_dev)
    back = lax.all_to_all(back, "seq", split_axis=0, concat_axis=0, tiled=True)
    back = back.reshape(owners * group, heads_dev, head_dim)
    attended = back[slot_of, head_cols]

    flat_out = attended.reshape(tok_dev, heads_dev * head_dim)
    return lax.psum_scatter(
        jnp.einsum("kc,tk->ct", out_weight, flat_out, preferred_element_type=jnp.float32).astype(
            jnp.bfloat16
        ),
        "head",
        scatter_dimension=0,
        tiled=True,
    )


def solution(mesh):
    return jax.shard_map(
        on_device,
        mesh=mesh,
        in_specs=(
            P("seq", "head", None),
            P("seq", "head", None),
            P("seq", "head", None),
            P("head", "seq", None),
            P("head", "seq", None),
            P("head", "seq", None),
            P("head", None),
        ),
        out_specs=P("head", "seq"),
        check_vma=False,
    )
```

```python
import functools

import jax
import jax.numpy as jnp
from jax import lax
from jax.experimental import pallas as pl
from jax.sharding import PartitionSpec as P

CLUSTERS = 256
MOST = 8


def place_kernel(slot_ref, q_ref, k_ref, v_ref, cent_ref, count_ref, out_ref, *, group):
    block, _, width = out_ref.shape
    heads_dev = slot_ref.shape[0]
    tok_dev, _ = q_ref.shape
    head_dim = width // heads_dev
    slots = block * group
    base = pl.program_id(0) * slots
    slot_ids = lax.broadcasted_iota(jnp.int32, (slots, tok_dev), 0) + base
    for h in range(heads_dev):
        onehot = (slot_ref[h] == slot_ids).astype(q_ref.dtype)
        cols = slice(h * head_dim, (h + 1) * head_dim)
        for kind, ref in enumerate((q_ref, k_ref, v_ref)):
            picked = jnp.dot(onehot, ref[:, cols], preferred_element_type=jnp.float32)
            out_ref[:, kind * group : (kind + 1) * group, cols] = picked.reshape(
                block, group, head_dim
            ).astype(out_ref.dtype)
    cent_rows = cent_ref.shape[0]
    out_ref[:, 3 * group : 3 * group + cent_rows, :] = jnp.broadcast_to(
        cent_ref[...][None], (block, cent_rows, width)
    )
    out_ref[:, 3 * group + cent_rows :, :] = count_ref[...]


def place(slot_rows, queries, keys, values, cent, counts, group, block):
    owners, count_rows, width = counts.shape
    tok_dev = queries.shape[0]
    cent_rows = cent.shape[0]
    rows = 3 * group + cent_rows + count_rows

    def whole(shape):
        return pl.BlockSpec(shape, lambda i: (0,) * len(shape))

    return pl.pallas_call(
        functools.partial(place_kernel, group=group),
        grid=(owners // block,),
        in_specs=[
            whole(slot_rows.shape),
            whole((tok_dev, width)),
            whole((tok_dev, width)),
            whole((tok_dev, width)),
            whole((cent_rows, width)),
            pl.BlockSpec((block, count_rows, width), lambda i: (i, 0, 0)),
        ],
        out_specs=pl.BlockSpec((block, rows, width), lambda i: (i, 0, 0)),
        out_shape=jax.ShapeDtypeStruct((owners, rows, width), queries.dtype),
    )(slot_rows, queries, keys, values, cent, counts)


def attention_kernel(q_ref, k_ref, v_ref, ck_ref, cv_ref, valid_ref, out_ref, *, scale):
    sources, depth, head_dim = q_ref.shape
    span = sources * depth

    def flat(ref):
        return ref[...].astype(jnp.float32).reshape(span, head_dim).astype(ref.dtype)

    q = flat(q_ref)
    k = flat(k_ref)
    v = flat(v_ref)
    ck = ck_ref[0, 0]
    cv = cv_ref[0, 0]
    contract = (((1,), (1,)), ((), ()))
    local = lax.dot_general(q, k, contract, preferred_element_type=jnp.float32) * scale
    row = lax.broadcasted_iota(jnp.int32, (span, span), 0)
    col = lax.broadcasted_iota(jnp.int32, (span, span), 1)
    allowed = (col <= row) & (valid_ref[0, 0] > 0.5)
    local = jnp.where(allowed, local, -1e30)
    memory = lax.dot_general(q, ck, contract, preferred_element_type=jnp.float32) * scale
    top = jnp.maximum(
        jnp.max(local, axis=1, keepdims=True), jnp.max(memory, axis=1, keepdims=True)
    )
    w_local = jnp.exp(local - top)
    w_memory = jnp.exp(memory - top)
    denom = jnp.sum(w_local, axis=1, keepdims=True) + jnp.sum(w_memory, axis=1, keepdims=True)
    numer = jnp.dot(w_local.astype(v.dtype), v, preferred_element_type=jnp.float32)
    numer = numer + jnp.dot(w_memory.astype(cv.dtype), cv, preferred_element_type=jnp.float32)
    result = (numer / denom).astype(out_ref.dtype).astype(jnp.float32)
    out_ref[...] = result.reshape(sources, depth, head_dim).astype(out_ref.dtype)


def cluster_attention(recv, cent, valid, scale, per_owner, heads_dev):
    sources, _, width = recv.shape
    head_dim = width // heads_dev
    clusters = cent.shape[2]

    def pick(kind):
        return pl.BlockSpec(
            (sources, MOST, head_dim), lambda c, h: (0, kind * per_owner + c, h)
        )

    def centroid(kind):
        return pl.BlockSpec((1, 1, clusters, head_dim), lambda c, h: (kind, h, 0, 0))

    return pl.pallas_call(
        functools.partial(attention_kernel, scale=scale),
        grid=(per_owner, heads_dev),
        in_specs=[
            pick(0),
            pick(1),
            pick(2),
            centroid(0),
            centroid(1),
            pl.BlockSpec((1, 1, 1, sources * MOST), lambda c, h: (c, h, 0, 0)),
        ],
        out_specs=pl.BlockSpec((sources, MOST, head_dim), lambda c, h: (0, c, h)),
        out_shape=jax.ShapeDtypeStruct((sources, per_owner * MOST, width), recv.dtype),
    )(recv, recv, recv, cent, cent, valid)


def on_device(queries, keys, values, clusters, cent_keys, cent_values, out_weight):
    tok_dev, heads_dev, head_dim = queries.shape
    owners = lax.axis_size("seq")
    per_owner = CLUSTERS // owners
    group = per_owner * MOST
    width = heads_dev * head_dim
    cent_rows = 2 * per_owner
    count_rows = 8
    scale = head_dim ** (-0.5)
    dtype = queries.dtype

    assign = clusters[:, :, 0]
    order = jnp.arange(tok_dev, dtype=jnp.int32)
    earlier = (assign[:, :, None] == assign[:, None, :]) & (
        order[None, None, :] < order[None, :, None]
    )
    rank = jnp.sum(earlier.astype(jnp.int32), axis=2)
    slot_of = (assign * MOST + rank).T
    head_cols = jnp.arange(heads_dev, dtype=jnp.int32)[None, :]

    counts = jnp.sum(
        (assign[:, :, None] == jnp.arange(CLUSTERS, dtype=jnp.int32)[None, None, :]).astype(jnp.int32),
        axis=1,
    )
    counts = jnp.transpose(counts.reshape(heads_dev, owners, per_owner), (1, 0, 2))
    counts = counts.reshape(owners, heads_dev * per_owner).astype(dtype)
    counts = jnp.pad(counts, ((0, 0), (0, count_rows * width - heads_dev * per_owner)))
    counts = counts.reshape(owners, count_rows, width)

    cent = jnp.stack([cent_keys, cent_values], axis=0).reshape(cent_rows, width)
    send = place(
        slot_of.T.reshape(heads_dev, 1, tok_dev),
        queries.reshape(tok_dev, width),
        keys.reshape(tok_dev, width),
        values.reshape(tok_dev, width),
        cent,
        counts,
        group,
        min(8, owners),
    )
    recv = lax.all_to_all(send, "seq", split_axis=0, concat_axis=0, tiled=True)

    span = owners * MOST
    cent_in = recv[:, 3 * group : 3 * group + cent_rows].reshape(
        owners, 2, heads_dev, per_owner, head_dim
    )
    cent_in = jnp.transpose(cent_in, (1, 2, 0, 3, 4)).reshape(2, heads_dev, CLUSTERS, head_dim)
    cnt = recv[:, 3 * group + cent_rows, : heads_dev * per_owner].astype(jnp.int32)
    cnt = cnt.reshape(owners, heads_dev, per_owner)
    depth = jnp.arange(MOST, dtype=jnp.int32)
    valid = depth[None, None, None, :] < jnp.transpose(cnt, (2, 1, 0))[..., None]
    valid = valid.astype(jnp.float32).reshape(per_owner, heads_dev, 1, span)

    back = cluster_attention(recv, cent_in, valid, scale, per_owner, heads_dev)
    back = lax.all_to_all(back, "seq", split_axis=0, concat_axis=0, tiled=True)
    back = back.reshape(owners * group, heads_dev, head_dim)
    attended = back[slot_of, head_cols]

    flat_out = attended.reshape(tok_dev, heads_dev * head_dim)
    return lax.psum_scatter(
        jnp.einsum("kc,tk->ct", out_weight, flat_out, preferred_element_type=jnp.float32).astype(
            jnp.bfloat16
        ),
        "head",
        scatter_dimension=0,
        tiled=True,
    )


def solution(mesh):
    return jax.shard_map(
        on_device,
        mesh=mesh,
        in_specs=(
            P("seq", "head", None),
            P("seq", "head", None),
            P("seq", "head", None),
            P("head", "seq", None),
            P("head", "seq", None),
            P("head", "seq", None),
            P("head", None),
        ),
        out_specs=P("head", "seq"),
        check_vma=False,
    )
```

```python
import functools

import jax
import jax.numpy as jnp
from jax import lax
from jax.experimental import pallas as pl
from jax.experimental.pallas import tpu as pltpu
from jax.sharding import PartitionSpec as P

CLUSTERS = 256
MOST = 8


def project_kernel(slot_ref, back_ref, wt_ref, out_ref, att_ref):
    tok_dev, heads_dev = slot_ref.shape
    slots, width = back_ref.shape
    head_dim = width // heads_dev

    @pl.when(pl.program_id(0) == 0)
    def _():
        ids = lax.broadcasted_iota(jnp.int32, (tok_dev, slots), 1)
        for h in range(heads_dev):
            cols = slice(h * head_dim, (h + 1) * head_dim)
            onehot = (slot_ref[:, h : h + 1] == ids).astype(back_ref.dtype)
            att_ref[:, cols] = jnp.dot(
                onehot, back_ref[:, cols], preferred_element_type=jnp.float32
            ).astype(att_ref.dtype)

    contract = (((1,), (1,)), ((), ()))
    out_ref[...] = lax.dot_general(
        wt_ref[...], att_ref[...], contract, preferred_element_type=jnp.float32
    ).astype(out_ref.dtype)


def project(slot_of, back, weight_t, steps):
    tok_dev, heads_dev = slot_of.shape
    slots, width = back.shape
    features = weight_t.shape[0]
    chunk = features // steps
    return pl.pallas_call(
        project_kernel,
        grid=(steps,),
        in_specs=[
            pl.BlockSpec((tok_dev, heads_dev), lambda i: (0, 0)),
            pl.BlockSpec((slots, width), lambda i: (0, 0)),
            pl.BlockSpec((chunk, width), lambda i: (i, 0)),
        ],
        out_specs=pl.BlockSpec((chunk, tok_dev), lambda i: (i, 0)),
        out_shape=jax.ShapeDtypeStruct((features, tok_dev), back.dtype),
        scratch_shapes=[pltpu.VMEM((tok_dev, width), back.dtype)],
        compiler_params=pltpu.CompilerParams(dimension_semantics=("arbitrary",)),
    )(slot_of, back, weight_t)


def place_kernel(slot_ref, q_ref, k_ref, v_ref, cent_ref, count_ref, out_ref, *, group):
    block, _, width = out_ref.shape
    heads_dev = slot_ref.shape[0]
    tok_dev, _ = q_ref.shape
    head_dim = width // heads_dev
    slots = block * group
    base = pl.program_id(0) * slots
    slot_ids = lax.broadcasted_iota(jnp.int32, (slots, tok_dev), 0) + base
    for h in range(heads_dev):
        onehot = (slot_ref[h] == slot_ids).astype(q_ref.dtype)
        cols = slice(h * head_dim, (h + 1) * head_dim)
        for kind, ref in enumerate((q_ref, k_ref, v_ref)):
            picked = jnp.dot(onehot, ref[:, cols], preferred_element_type=jnp.float32)
            out_ref[:, kind * group : (kind + 1) * group, cols] = picked.reshape(
                block, group, head_dim
            ).astype(out_ref.dtype)
    cent_rows = cent_ref.shape[0]
    out_ref[:, 3 * group : 3 * group + cent_rows, :] = jnp.broadcast_to(
        cent_ref[...][None], (block, cent_rows, width)
    )
    out_ref[:, 3 * group + cent_rows :, :] = count_ref[...]


def place(slot_rows, queries, keys, values, cent, counts, group, block):
    owners, count_rows, width = counts.shape
    tok_dev = queries.shape[0]
    cent_rows = cent.shape[0]
    rows = 3 * group + cent_rows + count_rows

    def whole(shape):
        return pl.BlockSpec(shape, lambda i: (0,) * len(shape))

    return pl.pallas_call(
        functools.partial(place_kernel, group=group),
        grid=(owners // block,),
        in_specs=[
            whole(slot_rows.shape),
            whole((tok_dev, width)),
            whole((tok_dev, width)),
            whole((tok_dev, width)),
            whole((cent_rows, width)),
            pl.BlockSpec((block, count_rows, width), lambda i: (i, 0, 0)),
        ],
        out_specs=pl.BlockSpec((block, rows, width), lambda i: (i, 0, 0)),
        out_shape=jax.ShapeDtypeStruct((owners, rows, width), queries.dtype),
    )(slot_rows, queries, keys, values, cent, counts)


def attention_kernel(q_ref, k_ref, v_ref, ck_ref, cv_ref, valid_ref, out_ref, *, scale):
    sources, depth, head_dim = q_ref.shape
    span = sources * depth

    def flat(ref):
        return ref[...].astype(jnp.float32).reshape(span, head_dim).astype(ref.dtype)

    q = flat(q_ref)
    k = flat(k_ref)
    v = flat(v_ref)
    ck = ck_ref[0, 0]
    cv = cv_ref[0, 0]
    contract = (((1,), (1,)), ((), ()))
    local = lax.dot_general(q, k, contract, preferred_element_type=jnp.float32) * scale
    row = lax.broadcasted_iota(jnp.int32, (span, span), 0)
    col = lax.broadcasted_iota(jnp.int32, (span, span), 1)
    allowed = (col <= row) & (valid_ref[0, 0] > 0.5)
    local = jnp.where(allowed, local, -1e30)
    memory = lax.dot_general(q, ck, contract, preferred_element_type=jnp.float32) * scale
    top = jnp.maximum(
        jnp.max(local, axis=1, keepdims=True), jnp.max(memory, axis=1, keepdims=True)
    )
    w_local = jnp.exp(local - top)
    w_memory = jnp.exp(memory - top)
    denom = jnp.sum(w_local, axis=1, keepdims=True) + jnp.sum(w_memory, axis=1, keepdims=True)
    numer = jnp.dot(w_local.astype(v.dtype), v, preferred_element_type=jnp.float32)
    numer = numer + jnp.dot(w_memory.astype(cv.dtype), cv, preferred_element_type=jnp.float32)
    result = (numer / denom).astype(out_ref.dtype).astype(jnp.float32)
    out_ref[...] = result.reshape(sources, depth, head_dim).astype(out_ref.dtype)


def cluster_attention(recv, cent, valid, scale, per_owner, heads_dev):
    sources, _, width = recv.shape
    head_dim = width // heads_dev
    clusters = cent.shape[2]

    def pick(kind):
        return pl.BlockSpec(
            (sources, MOST, head_dim), lambda c, h: (0, kind * per_owner + c, h)
        )

    def centroid(kind):
        return pl.BlockSpec((1, 1, clusters, head_dim), lambda c, h: (kind, h, 0, 0))

    return pl.pallas_call(
        functools.partial(attention_kernel, scale=scale),
        grid=(per_owner, heads_dev),
        in_specs=[
            pick(0),
            pick(1),
            pick(2),
            centroid(0),
            centroid(1),
            pl.BlockSpec((1, 1, 1, sources * MOST), lambda c, h: (c, h, 0, 0)),
        ],
        out_specs=pl.BlockSpec((sources, MOST, head_dim), lambda c, h: (0, c, h)),
        out_shape=jax.ShapeDtypeStruct((sources, per_owner * MOST, width), recv.dtype),
    )(recv, recv, recv, cent, cent, valid)


def on_device(queries, keys, values, clusters, cent_keys, cent_values, out_weight):
    tok_dev, heads_dev, head_dim = queries.shape
    owners = lax.axis_size("seq")
    per_owner = CLUSTERS // owners
    group = per_owner * MOST
    width = heads_dev * head_dim
    cent_rows = 2 * per_owner
    count_rows = 8
    scale = head_dim ** (-0.5)
    dtype = queries.dtype

    assign = clusters[:, :, 0]
    order = jnp.arange(tok_dev, dtype=jnp.int32)
    earlier = (assign[:, :, None] == assign[:, None, :]) & (
        order[None, None, :] < order[None, :, None]
    )
    rank = jnp.sum(earlier.astype(jnp.int32), axis=2)
    slot_of = (assign * MOST + rank).T
    head_cols = jnp.arange(heads_dev, dtype=jnp.int32)[None, :]

    counts = jnp.sum(
        (assign[:, :, None] == jnp.arange(CLUSTERS, dtype=jnp.int32)[None, None, :]).astype(jnp.int32),
        axis=1,
    )
    counts = jnp.transpose(counts.reshape(heads_dev, owners, per_owner), (1, 0, 2))
    counts = counts.reshape(owners, heads_dev * per_owner).astype(dtype)
    counts = jnp.pad(counts, ((0, 0), (0, count_rows * width - heads_dev * per_owner)))
    counts = counts.reshape(owners, count_rows, width)

    cent = jnp.stack([cent_keys, cent_values], axis=0).reshape(cent_rows, width)
    send = place(
        slot_of.T.reshape(heads_dev, 1, tok_dev),
        queries.reshape(tok_dev, width),
        keys.reshape(tok_dev, width),
        values.reshape(tok_dev, width),
        cent,
        counts,
        group,
        min(8, owners),
    )
    recv = lax.all_to_all(send, "seq", split_axis=0, concat_axis=0, tiled=True)

    span = owners * MOST
    cent_in = recv[:, 3 * group : 3 * group + cent_rows].reshape(
        owners, 2, heads_dev, per_owner, head_dim
    )
    cent_in = jnp.transpose(cent_in, (1, 2, 0, 3, 4)).reshape(2, heads_dev, CLUSTERS, head_dim)
    cnt = recv[:, 3 * group + cent_rows, : heads_dev * per_owner].astype(jnp.int32)
    cnt = cnt.reshape(owners, heads_dev, per_owner)
    depth = jnp.arange(MOST, dtype=jnp.int32)
    valid = depth[None, None, None, :] < jnp.transpose(cnt, (2, 1, 0))[..., None]
    valid = valid.astype(jnp.float32).reshape(per_owner, heads_dev, 1, span)

    back = cluster_attention(recv, cent_in, valid, scale, per_owner, heads_dev)
    back = lax.all_to_all(back, "seq", split_axis=0, concat_axis=0, tiled=True)
    back = back.reshape(owners * group, width)
    mixed = project(slot_of, back, out_weight.T, 4)
    return lax.psum_scatter(mixed, "head", scatter_dimension=0, tiled=True)


def solution(mesh):
    return jax.shard_map(
        on_device,
        mesh=mesh,
        in_specs=(
            P("seq", "head", None),
            P("seq", "head", None),
            P("seq", "head", None),
            P("head", "seq", None),
            P("head", "seq", None),
            P("head", "seq", None),
            P("head", None),
        ),
        out_specs=P("head", "seq"),
        check_vma=False,
    )
```

```python
import functools

import jax
import jax.numpy as jnp
from jax import lax
from jax.experimental import pallas as pl
from jax.experimental.pallas import tpu as pltpu
from jax.sharding import PartitionSpec as P

CLUSTERS = 256
MOST = 8


def project_kernel(slot_ref, back_ref, wt_ref, out_ref, att_ref):
    tok_dev, heads_dev = slot_ref.shape
    slots, width = back_ref.shape
    head_dim = width // heads_dev

    @pl.when(pl.program_id(0) == 0)
    def _():
        ids = lax.broadcasted_iota(jnp.int32, (tok_dev, slots), 1)
        for h in range(heads_dev):
            cols = slice(h * head_dim, (h + 1) * head_dim)
            onehot = (slot_ref[:, h : h + 1] == ids).astype(back_ref.dtype)
            att_ref[:, cols] = jnp.dot(
                onehot, back_ref[:, cols], preferred_element_type=jnp.float32
            ).astype(att_ref.dtype)

    contract = (((1,), (1,)), ((), ()))
    out_ref[...] = lax.dot_general(
        wt_ref[...], att_ref[...], contract, preferred_element_type=jnp.float32
    ).astype(out_ref.dtype)


def project(slot_of, back, weight_t, steps):
    tok_dev, heads_dev = slot_of.shape
    slots, width = back.shape
    features = weight_t.shape[0]
    chunk = features // steps
    return pl.pallas_call(
        project_kernel,
        grid=(steps,),
        in_specs=[
            pl.BlockSpec((tok_dev, heads_dev), lambda i: (0, 0)),
            pl.BlockSpec((slots, width), lambda i: (0, 0)),
            pl.BlockSpec((chunk, width), lambda i: (i, 0)),
        ],
        out_specs=pl.BlockSpec((chunk, tok_dev), lambda i: (i, 0)),
        out_shape=jax.ShapeDtypeStruct((features, tok_dev), back.dtype),
        scratch_shapes=[pltpu.VMEM((tok_dev, width), back.dtype)],
        compiler_params=pltpu.CompilerParams(dimension_semantics=("arbitrary",)),
    )(slot_of, back, weight_t)


def place_kernel(slot_ref, q_ref, k_ref, v_ref, cent_ref, count_ref, out_ref, *, group):
    block, _, width = out_ref.shape
    heads_dev = slot_ref.shape[0]
    tok_dev, _ = q_ref.shape
    head_dim = width // heads_dev
    slots = block * group
    base = pl.program_id(0) * slots
    slot_ids = lax.broadcasted_iota(jnp.int32, (slots, tok_dev), 0) + base
    for h in range(heads_dev):
        onehot = (slot_ref[h] == slot_ids).astype(q_ref.dtype)
        cols = slice(h * head_dim, (h + 1) * head_dim)
        for kind, ref in enumerate((q_ref, k_ref, v_ref)):
            picked = jnp.dot(onehot, ref[:, cols], preferred_element_type=jnp.float32)
            out_ref[:, kind * group : (kind + 1) * group, cols] = picked.reshape(
                block, group, head_dim
            ).astype(out_ref.dtype)
    cent_rows = cent_ref.shape[0]
    out_ref[:, 3 * group : 3 * group + cent_rows, :] = jnp.broadcast_to(
        cent_ref[...][None], (block, cent_rows, width)
    )
    out_ref[:, 3 * group + cent_rows :, :] = count_ref[...]


def place(slot_rows, queries, keys, values, cent, counts, group, block):
    owners, count_rows, width = counts.shape
    tok_dev = queries.shape[0]
    cent_rows = cent.shape[0]
    rows = 3 * group + cent_rows + count_rows

    def whole(shape):
        return pl.BlockSpec(shape, lambda i: (0,) * len(shape))

    return pl.pallas_call(
        functools.partial(place_kernel, group=group),
        grid=(owners // block,),
        in_specs=[
            whole(slot_rows.shape),
            whole((tok_dev, width)),
            whole((tok_dev, width)),
            whole((tok_dev, width)),
            whole((cent_rows, width)),
            pl.BlockSpec((block, count_rows, width), lambda i: (i, 0, 0)),
        ],
        out_specs=pl.BlockSpec((block, rows, width), lambda i: (i, 0, 0)),
        out_shape=jax.ShapeDtypeStruct((owners, rows, width), queries.dtype),
    )(slot_rows, queries, keys, values, cent, counts)


def attention_kernel(q_ref, k_ref, v_ref, ck_ref, cv_ref, valid_ref, out_ref, *, scale):
    sources, depth, head_dim = q_ref.shape
    span = sources * depth

    def flat(ref):
        return ref[...].astype(jnp.float32).reshape(span, head_dim).astype(ref.dtype)

    q = flat(q_ref)
    k = flat(k_ref)
    v = flat(v_ref)
    ck = ck_ref[0, 0]
    cv = cv_ref[0, 0]
    contract = (((1,), (1,)), ((), ()))
    memory_all = lax.dot_general(q, ck, contract, preferred_element_type=jnp.float32) * scale
    valid = valid_ref[0, 0] > 0.5
    rows = min(128, span)
    for b in range(span // rows):
        first = b * rows
        seen = first + rows
        local = (
            lax.dot_general(q[first:seen], k[:seen], contract, preferred_element_type=jnp.float32)
            * scale
        )
        row = lax.broadcasted_iota(jnp.int32, (rows, seen), 0) + first
        col = lax.broadcasted_iota(jnp.int32, (rows, seen), 1)
        allowed = (col <= row) & valid[:, :seen]
        local = jnp.where(allowed, local, -1e30)
        memory = memory_all[first:seen]
        top = jnp.maximum(
            jnp.max(local, axis=1, keepdims=True), jnp.max(memory, axis=1, keepdims=True)
        )
        w_local = jnp.exp(local - top)
        w_memory = jnp.exp(memory - top)
        denom = jnp.sum(w_local, axis=1, keepdims=True) + jnp.sum(
            w_memory, axis=1, keepdims=True
        )
        numer = jnp.dot(w_local.astype(v.dtype), v[:seen], preferred_element_type=jnp.float32)
        numer = numer + jnp.dot(
            w_memory.astype(cv.dtype), cv, preferred_element_type=jnp.float32
        )
        result = (numer / denom).astype(out_ref.dtype).astype(jnp.float32)
        out_ref[first // depth : seen // depth] = result.reshape(
            rows // depth, depth, head_dim
        ).astype(out_ref.dtype)


def cluster_attention(recv, cent, valid, scale, per_owner, heads_dev):
    sources, _, width = recv.shape
    head_dim = width // heads_dev
    clusters = cent.shape[2]

    def pick(kind):
        return pl.BlockSpec(
            (sources, MOST, head_dim), lambda c, h: (0, kind * per_owner + c, h)
        )

    def centroid(kind):
        return pl.BlockSpec((1, 1, clusters, head_dim), lambda c, h: (kind, h, 0, 0))

    return pl.pallas_call(
        functools.partial(attention_kernel, scale=scale),
        grid=(per_owner, heads_dev),
        in_specs=[
            pick(0),
            pick(1),
            pick(2),
            centroid(0),
            centroid(1),
            pl.BlockSpec((1, 1, 1, sources * MOST), lambda c, h: (c, h, 0, 0)),
        ],
        out_specs=pl.BlockSpec((sources, MOST, head_dim), lambda c, h: (0, c, h)),
        out_shape=jax.ShapeDtypeStruct((sources, per_owner * MOST, width), recv.dtype),
    )(recv, recv, recv, cent, cent, valid)


def on_device(queries, keys, values, clusters, cent_keys, cent_values, out_weight):
    tok_dev, heads_dev, head_dim = queries.shape
    owners = lax.axis_size("seq")
    per_owner = CLUSTERS // owners
    group = per_owner * MOST
    width = heads_dev * head_dim
    cent_rows = 2 * per_owner
    count_rows = 8
    scale = head_dim ** (-0.5)
    dtype = queries.dtype

    assign = clusters[:, :, 0]
    order = jnp.arange(tok_dev, dtype=jnp.int32)
    earlier = (assign[:, :, None] == assign[:, None, :]) & (
        order[None, None, :] < order[None, :, None]
    )
    rank = jnp.sum(earlier.astype(jnp.int32), axis=2)
    slot_of = (assign * MOST + rank).T
    head_cols = jnp.arange(heads_dev, dtype=jnp.int32)[None, :]

    counts = jnp.sum(
        (assign[:, :, None] == jnp.arange(CLUSTERS, dtype=jnp.int32)[None, None, :]).astype(jnp.int32),
        axis=1,
    )
    counts = jnp.transpose(counts.reshape(heads_dev, owners, per_owner), (1, 0, 2))
    counts = counts.reshape(owners, heads_dev * per_owner).astype(dtype)
    counts = jnp.pad(counts, ((0, 0), (0, count_rows * width - heads_dev * per_owner)))
    counts = counts.reshape(owners, count_rows, width)

    cent = jnp.stack([cent_keys, cent_values], axis=0).reshape(cent_rows, width)
    send = place(
        slot_of.T.reshape(heads_dev, 1, tok_dev),
        queries.reshape(tok_dev, width),
        keys.reshape(tok_dev, width),
        values.reshape(tok_dev, width),
        cent,
        counts,
        group,
        min(8, owners),
    )
    recv = lax.all_to_all(send, "seq", split_axis=0, concat_axis=0, tiled=True)

    span = owners * MOST
    cent_in = recv[:, 3 * group : 3 * group + cent_rows].reshape(
        owners, 2, heads_dev, per_owner, head_dim
    )
    cent_in = jnp.transpose(cent_in, (1, 2, 0, 3, 4)).reshape(2, heads_dev, CLUSTERS, head_dim)
    cnt = recv[:, 3 * group + cent_rows, : heads_dev * per_owner].astype(jnp.int32)
    cnt = cnt.reshape(owners, heads_dev, per_owner)
    depth = jnp.arange(MOST, dtype=jnp.int32)
    valid = depth[None, None, None, :] < jnp.transpose(cnt, (2, 1, 0))[..., None]
    valid = valid.astype(jnp.float32).reshape(per_owner, heads_dev, 1, span)

    back = cluster_attention(recv, cent_in, valid, scale, per_owner, heads_dev)
    back = lax.all_to_all(back, "seq", split_axis=0, concat_axis=0, tiled=True)
    back = back.reshape(owners * group, width)
    mixed = project(slot_of, back, out_weight.T, 4)
    return lax.psum_scatter(mixed, "head", scatter_dimension=0, tiled=True)


def solution(mesh):
    return jax.shard_map(
        on_device,
        mesh=mesh,
        in_specs=(
            P("seq", "head", None),
            P("seq", "head", None),
            P("seq", "head", None),
            P("head", "seq", None),
            P("head", "seq", None),
            P("head", "seq", None),
            P("head", None),
        ),
        out_specs=P("head", "seq"),
        check_vma=False,
    )
```

```python
import functools

import jax
import jax.numpy as jnp
from jax import lax
from jax.experimental import pallas as pl
from jax.experimental.pallas import tpu as pltpu
from jax.sharding import PartitionSpec as P

CLUSTERS = 256
MOST = 8


def project_kernel(slot_ref, back_ref, wt_ref, out_ref, att_ref):
    tok_dev, heads_dev = slot_ref.shape
    slots, width = back_ref.shape
    head_dim = width // heads_dev

    @pl.when(pl.program_id(0) == 0)
    def _():
        ids = lax.broadcasted_iota(jnp.int32, (tok_dev, slots), 1)
        for h in range(heads_dev):
            cols = slice(h * head_dim, (h + 1) * head_dim)
            onehot = (slot_ref[:, h : h + 1] == ids).astype(back_ref.dtype)
            att_ref[:, cols] = jnp.dot(
                onehot, back_ref[:, cols], preferred_element_type=jnp.float32
            ).astype(att_ref.dtype)

    contract = (((1,), (1,)), ((), ()))
    out_ref[...] = lax.dot_general(
        wt_ref[...], att_ref[...], contract, preferred_element_type=jnp.float32
    ).astype(out_ref.dtype)


def project(slot_of, back, weight_t, steps):
    tok_dev, heads_dev = slot_of.shape
    slots, width = back.shape
    features = weight_t.shape[0]
    chunk = features // steps
    return pl.pallas_call(
        project_kernel,
        grid=(steps,),
        in_specs=[
            pl.BlockSpec((tok_dev, heads_dev), lambda i: (0, 0)),
            pl.BlockSpec((slots, width), lambda i: (0, 0)),
            pl.BlockSpec((chunk, width), lambda i: (i, 0)),
        ],
        out_specs=pl.BlockSpec((chunk, tok_dev), lambda i: (i, 0)),
        out_shape=jax.ShapeDtypeStruct((features, tok_dev), back.dtype),
        scratch_shapes=[pltpu.VMEM((tok_dev, width), back.dtype)],
        compiler_params=pltpu.CompilerParams(dimension_semantics=("arbitrary",)),
    )(slot_of, back, weight_t)


def place_kernel(slot_ref, q_ref, k_ref, v_ref, cent_ref, count_ref, out_ref, *, group):
    block, _, width = out_ref.shape
    heads_dev = slot_ref.shape[0]
    tok_dev, _ = q_ref.shape
    head_dim = width // heads_dev
    slots = block * group
    base = pl.program_id(0) * slots
    slot_ids = lax.broadcasted_iota(jnp.int32, (slots, tok_dev), 0) + base
    for h in range(heads_dev):
        onehot = (slot_ref[h] == slot_ids).astype(q_ref.dtype)
        cols = slice(h * head_dim, (h + 1) * head_dim)
        for kind, ref in enumerate((q_ref, k_ref, v_ref)):
            picked = jnp.dot(onehot, ref[:, cols], preferred_element_type=jnp.float32)
            out_ref[:, kind * group : (kind + 1) * group, cols] = picked.reshape(
                block, group, head_dim
            ).astype(out_ref.dtype)
    cent_rows = cent_ref.shape[0]
    out_ref[:, 3 * group : 3 * group + cent_rows, :] = jnp.broadcast_to(
        cent_ref[...][None], (block, cent_rows, width)
    )
    out_ref[:, 3 * group + cent_rows :, :] = count_ref[...]


def place(slot_rows, queries, keys, values, cent, counts, group, block):
    owners, count_rows, width = counts.shape
    tok_dev = queries.shape[0]
    cent_rows = cent.shape[0]
    rows = 3 * group + cent_rows + count_rows

    def whole(shape):
        return pl.BlockSpec(shape, lambda i: (0,) * len(shape))

    return pl.pallas_call(
        functools.partial(place_kernel, group=group),
        grid=(owners // block,),
        in_specs=[
            whole(slot_rows.shape),
            whole((tok_dev, width)),
            whole((tok_dev, width)),
            whole((tok_dev, width)),
            whole((cent_rows, width)),
            pl.BlockSpec((block, count_rows, width), lambda i: (i, 0, 0)),
        ],
        out_specs=pl.BlockSpec((block, rows, width), lambda i: (i, 0, 0)),
        out_shape=jax.ShapeDtypeStruct((owners, rows, width), queries.dtype),
    )(slot_rows, queries, keys, values, cent, counts)


def attention_kernel(q_ref, k_ref, v_ref, ck_ref, cv_ref, valid_ref, out_ref, *, scale):
    sources, depth, width = q_ref.shape
    heads_dev = ck_ref.shape[1]
    head_dim = width // heads_dev
    span = sources * depth

    def flat(ref):
        return ref[...].astype(jnp.float32).reshape(span, width).astype(ref.dtype)

    q_all = flat(q_ref)
    k_all = flat(k_ref)
    v_all = flat(v_ref)
    contract = (((1,), (1,)), ((), ()))
    row = lax.broadcasted_iota(jnp.int32, (span, span), 0)
    col = lax.broadcasted_iota(jnp.int32, (span, span), 1)
    for h in range(heads_dev):
        cols = slice(h * head_dim, (h + 1) * head_dim)
        q = q_all[:, cols]
        k = k_all[:, cols]
        v = v_all[:, cols]
        ck = ck_ref[0, h]
        cv = cv_ref[0, h]
        local = lax.dot_general(q, k, contract, preferred_element_type=jnp.float32) * scale
        allowed = (col <= row) & (valid_ref[0, h] > 0.5)
        local = jnp.where(allowed, local, -1e30)
        memory = lax.dot_general(q, ck, contract, preferred_element_type=jnp.float32) * scale
        top = jnp.maximum(
            jnp.max(local, axis=1, keepdims=True), jnp.max(memory, axis=1, keepdims=True)
        )
        w_local = jnp.exp(local - top)
        w_memory = jnp.exp(memory - top)
        denom = jnp.sum(w_local, axis=1, keepdims=True) + jnp.sum(
            w_memory, axis=1, keepdims=True
        )
        numer = jnp.dot(w_local.astype(v.dtype), v, preferred_element_type=jnp.float32)
        numer = numer + jnp.dot(
            w_memory.astype(cv.dtype), cv, preferred_element_type=jnp.float32
        )
        result = (numer / denom).astype(out_ref.dtype).astype(jnp.float32)
        out_ref[:, :, cols] = result.reshape(sources, depth, head_dim).astype(out_ref.dtype)


def cluster_attention(recv, cent, valid, scale, per_owner, heads_dev):
    sources, _, width = recv.shape
    head_dim = width // heads_dev
    clusters = cent.shape[2]

    def pick(kind):
        return pl.BlockSpec((sources, MOST, width), lambda c: (0, kind * per_owner + c, 0))

    def centroid(kind):
        return pl.BlockSpec((1, heads_dev, clusters, head_dim), lambda c: (kind, 0, 0, 0))

    return pl.pallas_call(
        functools.partial(attention_kernel, scale=scale),
        grid=(per_owner,),
        in_specs=[
            pick(0),
            pick(1),
            pick(2),
            centroid(0),
            centroid(1),
            pl.BlockSpec((1, heads_dev, 1, sources * MOST), lambda c: (c, 0, 0, 0)),
        ],
        out_specs=pl.BlockSpec((sources, MOST, width), lambda c: (0, c, 0)),
        out_shape=jax.ShapeDtypeStruct((sources, per_owner * MOST, width), recv.dtype),
    )(recv, recv, recv, cent, cent, valid)


def on_device(queries, keys, values, clusters, cent_keys, cent_values, out_weight):
    tok_dev, heads_dev, head_dim = queries.shape
    owners = lax.axis_size("seq")
    per_owner = CLUSTERS // owners
    group = per_owner * MOST
    width = heads_dev * head_dim
    cent_rows = 2 * per_owner
    count_rows = 8
    scale = head_dim ** (-0.5)
    dtype = queries.dtype

    assign = clusters[:, :, 0]
    order = jnp.arange(tok_dev, dtype=jnp.int32)
    earlier = (assign[:, :, None] == assign[:, None, :]) & (
        order[None, None, :] < order[None, :, None]
    )
    rank = jnp.sum(earlier.astype(jnp.int32), axis=2)
    slot_of = (assign * MOST + rank).T
    head_cols = jnp.arange(heads_dev, dtype=jnp.int32)[None, :]

    counts = jnp.sum(
        (assign[:, :, None] == jnp.arange(CLUSTERS, dtype=jnp.int32)[None, None, :]).astype(jnp.int32),
        axis=1,
    )
    counts = jnp.transpose(counts.reshape(heads_dev, owners, per_owner), (1, 0, 2))
    counts = counts.reshape(owners, heads_dev * per_owner).astype(dtype)
    counts = jnp.pad(counts, ((0, 0), (0, count_rows * width - heads_dev * per_owner)))
    counts = counts.reshape(owners, count_rows, width)

    cent = jnp.stack([cent_keys, cent_values], axis=0).reshape(cent_rows, width)
    send = place(
        slot_of.T.reshape(heads_dev, 1, tok_dev),
        queries.reshape(tok_dev, width),
        keys.reshape(tok_dev, width),
        values.reshape(tok_dev, width),
        cent,
        counts,
        group,
        min(8, owners),
    )
    recv = lax.all_to_all(send, "seq", split_axis=0, concat_axis=0, tiled=True)

    span = owners * MOST
    cent_in = recv[:, 3 * group : 3 * group + cent_rows].reshape(
        owners, 2, heads_dev, per_owner, head_dim
    )
    cent_in = jnp.transpose(cent_in, (1, 2, 0, 3, 4)).reshape(2, heads_dev, CLUSTERS, head_dim)
    cnt = recv[:, 3 * group + cent_rows, : heads_dev * per_owner].astype(jnp.int32)
    cnt = cnt.reshape(owners, heads_dev, per_owner)
    depth = jnp.arange(MOST, dtype=jnp.int32)
    valid = depth[None, None, None, :] < jnp.transpose(cnt, (2, 1, 0))[..., None]
    valid = valid.astype(jnp.float32).reshape(per_owner, heads_dev, 1, span)

    back = cluster_attention(recv, cent_in, valid, scale, per_owner, heads_dev)
    back = lax.all_to_all(back, "seq", split_axis=0, concat_axis=0, tiled=True)
    back = back.reshape(owners * group, width)
    mixed = project(slot_of, back, out_weight.T, 4)
    return lax.psum_scatter(mixed, "head", scatter_dimension=0, tiled=True)


def solution(mesh):
    return jax.shard_map(
        on_device,
        mesh=mesh,
        in_specs=(
            P("seq", "head", None),
            P("seq", "head", None),
            P("seq", "head", None),
            P("head", "seq", None),
            P("head", "seq", None),
            P("head", "seq", None),
            P("head", None),
        ),
        out_specs=P("head", "seq"),
        check_vma=False,
    )
```

```python
import functools

import jax
import jax.numpy as jnp
from jax import lax
from jax.experimental import pallas as pl
from jax.experimental.pallas import tpu as pltpu
from jax.sharding import PartitionSpec as P

CLUSTERS = 256
MOST = 8


def project_kernel(slot_ref, back_ref, wt_ref, out_ref, att_ref):
    tok_dev, heads_dev = slot_ref.shape
    slots, width = back_ref.shape
    head_dim = width // heads_dev

    @pl.when(pl.program_id(0) == 0)
    def _():
        ids = lax.broadcasted_iota(jnp.int32, (tok_dev, slots), 1)
        for h in range(heads_dev):
            cols = slice(h * head_dim, (h + 1) * head_dim)
            onehot = (slot_ref[:, h : h + 1] == ids).astype(back_ref.dtype)
            att_ref[:, cols] = jnp.dot(
                onehot, back_ref[:, cols], preferred_element_type=jnp.float32
            ).astype(att_ref.dtype)

    contract = (((1,), (1,)), ((), ()))
    out_ref[...] = lax.dot_general(
        wt_ref[...], att_ref[...], contract, preferred_element_type=jnp.float32
    ).astype(out_ref.dtype)


def project(slot_of, back, weight_t, steps):
    tok_dev, heads_dev = slot_of.shape
    slots, width = back.shape
    features = weight_t.shape[0]
    chunk = features // steps
    return pl.pallas_call(
        project_kernel,
        grid=(steps,),
        in_specs=[
            pl.BlockSpec((tok_dev, heads_dev), lambda i: (0, 0)),
            pl.BlockSpec((slots, width), lambda i: (0, 0)),
            pl.BlockSpec((chunk, width), lambda i: (i, 0)),
        ],
        out_specs=pl.BlockSpec((chunk, tok_dev), lambda i: (i, 0)),
        out_shape=jax.ShapeDtypeStruct((features, tok_dev), back.dtype),
        scratch_shapes=[pltpu.VMEM((tok_dev, width), back.dtype)],
        compiler_params=pltpu.CompilerParams(dimension_semantics=("arbitrary",)),
    )(slot_of, back, weight_t)


def place_kernel(slot_ref, q_ref, k_ref, v_ref, cent_ref, count_ref, out_ref, *, group):
    block, _, width = out_ref.shape
    heads_dev = slot_ref.shape[0]
    tok_dev, _ = q_ref.shape
    head_dim = width // heads_dev
    slots = block * group
    base = pl.program_id(0) * slots
    slot_ids = lax.broadcasted_iota(jnp.int32, (slots, tok_dev), 0) + base
    for h in range(heads_dev):
        onehot = (slot_ref[h] == slot_ids).astype(q_ref.dtype)
        cols = slice(h * head_dim, (h + 1) * head_dim)
        for kind, ref in enumerate((q_ref, k_ref, v_ref)):
            picked = jnp.dot(onehot, ref[:, cols], preferred_element_type=jnp.float32)
            out_ref[:, kind * group : (kind + 1) * group, cols] = picked.reshape(
                block, group, head_dim
            ).astype(out_ref.dtype)
    cent_rows = cent_ref.shape[0]
    out_ref[:, 3 * group : 3 * group + cent_rows, :] = jnp.broadcast_to(
        cent_ref[...][None], (block, cent_rows, width)
    )
    out_ref[:, 3 * group + cent_rows :, :] = count_ref[...]


def place(slot_rows, queries, keys, values, cent, counts, group, block):
    owners, count_rows, width = counts.shape
    tok_dev = queries.shape[0]
    cent_rows = cent.shape[0]
    rows = 3 * group + cent_rows + count_rows

    def whole(shape):
        return pl.BlockSpec(shape, lambda i: (0,) * len(shape))

    return pl.pallas_call(
        functools.partial(place_kernel, group=group),
        grid=(owners // block,),
        in_specs=[
            whole(slot_rows.shape),
            whole((tok_dev, width)),
            whole((tok_dev, width)),
            whole((tok_dev, width)),
            whole((cent_rows, width)),
            pl.BlockSpec((block, count_rows, width), lambda i: (i, 0, 0)),
        ],
        out_specs=pl.BlockSpec((block, rows, width), lambda i: (i, 0, 0)),
        out_shape=jax.ShapeDtypeStruct((owners, rows, width), queries.dtype),
    )(slot_rows, queries, keys, values, cent, counts)


def attention_kernel(q_ref, k_ref, v_ref, ck_ref, cv_ref, valid_ref, out_ref, *, scale):
    sources, depth, width = q_ref.shape
    heads_dev = ck_ref.shape[1]
    head_dim = width // heads_dev
    span = sources * depth

    def flat(ref):
        return ref[...].astype(jnp.float32).reshape(span, width).astype(ref.dtype)

    q_all = flat(q_ref)
    k_all = flat(k_ref)
    v_all = flat(v_ref)
    contract = (((1,), (1,)), ((), ()))
    row = lax.broadcasted_iota(jnp.int32, (span, span), 0)
    col = lax.broadcasted_iota(jnp.int32, (span, span), 1)
    for h in range(heads_dev):
        cols = slice(h * head_dim, (h + 1) * head_dim)
        q = q_all[:, cols]
        k = k_all[:, cols]
        v = v_all[:, cols]
        ck = ck_ref[0, h]
        cv = cv_ref[0, h]
        local = lax.dot_general(q, k, contract, preferred_element_type=jnp.float32) * scale
        allowed = (col <= row) & (valid_ref[0, h] > 0.5)
        local = jnp.where(allowed, local, -1e30)
        memory = lax.dot_general(q, ck, contract, preferred_element_type=jnp.float32) * scale
        top = jnp.maximum(
            jnp.max(local, axis=1, keepdims=True), jnp.max(memory, axis=1, keepdims=True)
        )
        w_local = jnp.exp(local - top)
        w_memory = jnp.exp(memory - top)
        denom = jnp.sum(w_local, axis=1, keepdims=True) + jnp.sum(
            w_memory, axis=1, keepdims=True
        )
        numer = jnp.dot(w_local.astype(v.dtype), v, preferred_element_type=jnp.float32)
        numer = numer + jnp.dot(
            w_memory.astype(cv.dtype), cv, preferred_element_type=jnp.float32
        )
        result = (numer / denom).astype(out_ref.dtype).astype(jnp.float32)
        out_ref[:, :, cols] = result.reshape(sources, depth, head_dim).astype(out_ref.dtype)


def cluster_attention(recv, cent, valid, scale, per_owner, heads_dev):
    sources, _, width = recv.shape
    head_dim = width // heads_dev
    clusters = cent.shape[2]

    def pick(kind):
        return pl.BlockSpec((sources, MOST, width), lambda c: (0, kind * per_owner + c, 0))

    def centroid(kind):
        return pl.BlockSpec((1, heads_dev, clusters, head_dim), lambda c: (kind, 0, 0, 0))

    return pl.pallas_call(
        functools.partial(attention_kernel, scale=scale),
        grid=(per_owner,),
        in_specs=[
            pick(0),
            pick(1),
            pick(2),
            centroid(0),
            centroid(1),
            pl.BlockSpec((1, heads_dev, 1, sources * MOST), lambda c: (c, 0, 0, 0)),
        ],
        out_specs=pl.BlockSpec((sources, MOST, width), lambda c: (0, c, 0)),
        out_shape=jax.ShapeDtypeStruct((sources, per_owner * MOST, width), recv.dtype),
    )(recv, recv, recv, cent, cent, valid)


def on_device(queries, keys, values, clusters, cent_keys, cent_values, out_weight):
    tok_dev, heads_dev, head_dim = queries.shape
    owners = lax.axis_size("seq")
    per_owner = CLUSTERS // owners
    group = per_owner * MOST
    width = heads_dev * head_dim
    cent_rows = 2 * per_owner
    count_rows = 8
    scale = head_dim ** (-0.5)
    dtype = queries.dtype

    assign = clusters[:, :, 0]
    order = jnp.arange(tok_dev, dtype=jnp.int32)
    earlier = (assign[:, :, None] == assign[:, None, :]) & (
        order[None, None, :] < order[None, :, None]
    )
    rank = jnp.sum(earlier.astype(jnp.int32), axis=2)
    slot_of = (assign * MOST + rank).T
    head_cols = jnp.arange(heads_dev, dtype=jnp.int32)[None, :]

    counts = jnp.sum(
        (assign[:, :, None] == jnp.arange(CLUSTERS, dtype=jnp.int32)[None, None, :]).astype(jnp.int32),
        axis=1,
    )
    counts = jnp.transpose(counts.reshape(heads_dev, owners, per_owner), (1, 0, 2))
    counts = counts.reshape(owners, heads_dev * per_owner).astype(dtype)
    counts = jnp.pad(counts, ((0, 0), (0, count_rows * width - heads_dev * per_owner)))
    counts = counts.reshape(owners, count_rows, width)

    cent = jnp.stack([cent_keys, cent_values], axis=0).reshape(cent_rows, width)
    send = place(
        slot_of.T.reshape(heads_dev, 1, tok_dev),
        queries.reshape(tok_dev, width),
        keys.reshape(tok_dev, width),
        values.reshape(tok_dev, width),
        cent,
        counts,
        group,
        min(16, owners),
    )
    recv = lax.all_to_all(send, "seq", split_axis=0, concat_axis=0, tiled=True)

    span = owners * MOST
    cent_in = recv[:, 3 * group : 3 * group + cent_rows].reshape(
        owners, 2, heads_dev, per_owner, head_dim
    )
    cent_in = jnp.transpose(cent_in, (1, 2, 0, 3, 4)).reshape(2, heads_dev, CLUSTERS, head_dim)
    cnt = recv[:, 3 * group + cent_rows, : heads_dev * per_owner].astype(jnp.int32)
    cnt = cnt.reshape(owners, heads_dev, per_owner)
    depth = jnp.arange(MOST, dtype=jnp.int32)
    valid = depth[None, None, None, :] < jnp.transpose(cnt, (2, 1, 0))[..., None]
    valid = valid.astype(jnp.float32).reshape(per_owner, heads_dev, 1, span)

    back = cluster_attention(recv, cent_in, valid, scale, per_owner, heads_dev)
    back = lax.all_to_all(back, "seq", split_axis=0, concat_axis=0, tiled=True)
    back = back.reshape(owners * group, width)
    mixed = project(slot_of, back, out_weight.T, 4)
    return lax.psum_scatter(mixed, "head", scatter_dimension=0, tiled=True)


def solution(mesh):
    return jax.shard_map(
        on_device,
        mesh=mesh,
        in_specs=(
            P("seq", "head", None),
            P("seq", "head", None),
            P("seq", "head", None),
            P("head", "seq", None),
            P("head", "seq", None),
            P("head", "seq", None),
            P("head", None),
        ),
        out_specs=P("head", "seq"),
        check_vma=False,
    )
```

```python
import functools

import jax
import jax.numpy as jnp
from jax import lax
from jax.experimental import pallas as pl
from jax.experimental.pallas import tpu as pltpu
from jax.sharding import PartitionSpec as P

CLUSTERS = 256
MOST = 8


def project_kernel(slot_ref, back_ref, wt_ref, out_ref, att_ref):
    tok_dev, heads_dev = slot_ref.shape
    slots, width = back_ref.shape
    head_dim = width // heads_dev

    @pl.when(pl.program_id(0) == 0)
    def _():
        ids = lax.broadcasted_iota(jnp.int32, (tok_dev, slots), 1)
        for h in range(heads_dev):
            cols = slice(h * head_dim, (h + 1) * head_dim)
            onehot = (slot_ref[:, h : h + 1] == ids).astype(back_ref.dtype)
            att_ref[:, cols] = jnp.dot(
                onehot, back_ref[:, cols], preferred_element_type=jnp.float32
            ).astype(att_ref.dtype)

    contract = (((1,), (1,)), ((), ()))
    out_ref[...] = lax.dot_general(
        wt_ref[...], att_ref[...], contract, preferred_element_type=jnp.float32
    ).astype(out_ref.dtype)


def project(slot_of, back, weight_t, steps):
    tok_dev, heads_dev = slot_of.shape
    slots, width = back.shape
    features = weight_t.shape[0]
    chunk = features // steps
    return pl.pallas_call(
        project_kernel,
        grid=(steps,),
        in_specs=[
            pl.BlockSpec((tok_dev, heads_dev), lambda i: (0, 0)),
            pl.BlockSpec((slots, width), lambda i: (0, 0)),
            pl.BlockSpec((chunk, width), lambda i: (i, 0)),
        ],
        out_specs=pl.BlockSpec((chunk, tok_dev), lambda i: (i, 0)),
        out_shape=jax.ShapeDtypeStruct((features, tok_dev), back.dtype),
        scratch_shapes=[pltpu.VMEM((tok_dev, width), back.dtype)],
        compiler_params=pltpu.CompilerParams(dimension_semantics=("arbitrary",)),
    )(slot_of, back, weight_t)


def place_kernel(slot_ref, q_ref, k_ref, v_ref, cent_ref, count_ref, out_ref, *, group):
    block, _, width = out_ref.shape
    heads_dev = slot_ref.shape[0]
    tok_dev, _ = q_ref.shape
    head_dim = width // heads_dev
    slots = block * group
    base = pl.program_id(0) * slots
    slot_ids = lax.broadcasted_iota(jnp.int32, (slots, tok_dev), 0) + base
    for h in range(heads_dev):
        onehot = (slot_ref[h] == slot_ids).astype(q_ref.dtype)
        cols = slice(h * head_dim, (h + 1) * head_dim)
        for kind, ref in enumerate((q_ref, k_ref, v_ref)):
            picked = jnp.dot(onehot, ref[:, cols], preferred_element_type=jnp.float32)
            out_ref[:, kind * group : (kind + 1) * group, cols] = picked.reshape(
                block, group, head_dim
            ).astype(out_ref.dtype)
    cent_rows = cent_ref.shape[0]
    out_ref[:, 3 * group : 3 * group + cent_rows, :] = jnp.broadcast_to(
        cent_ref[...][None], (block, cent_rows, width)
    )
    out_ref[:, 3 * group + cent_rows :, :] = count_ref[...]


def place(slot_rows, queries, keys, values, cent, counts, group, block):
    owners, count_rows, width = counts.shape
    tok_dev = queries.shape[0]
    cent_rows = cent.shape[0]
    rows = 3 * group + cent_rows + count_rows

    def whole(shape):
        return pl.BlockSpec(shape, lambda i: (0,) * len(shape))

    return pl.pallas_call(
        functools.partial(place_kernel, group=group),
        grid=(owners // block,),
        in_specs=[
            whole(slot_rows.shape),
            whole((tok_dev, width)),
            whole((tok_dev, width)),
            whole((tok_dev, width)),
            whole((cent_rows, width)),
            pl.BlockSpec((block, count_rows, width), lambda i: (i, 0, 0)),
        ],
        out_specs=pl.BlockSpec((block, rows, width), lambda i: (i, 0, 0)),
        out_shape=jax.ShapeDtypeStruct((owners, rows, width), queries.dtype),
    )(slot_rows, queries, keys, values, cent, counts)


def attention_kernel(q_ref, k_ref, v_ref, ck_ref, cv_ref, valid_ref, out_ref, *, scale):
    sources, depth, width = q_ref.shape
    heads_dev = ck_ref.shape[1]
    head_dim = width // heads_dev
    span = sources * depth

    def flat(ref):
        return ref[...].astype(jnp.float32).reshape(span, width).astype(ref.dtype)

    q_all = flat(q_ref)
    k_all = flat(k_ref)
    v_all = flat(v_ref)
    contract = (((1,), (1,)), ((), ()))
    row = lax.broadcasted_iota(jnp.int32, (span, span), 0)
    col = lax.broadcasted_iota(jnp.int32, (span, span), 1)
    for h in range(heads_dev):
        cols = slice(h * head_dim, (h + 1) * head_dim)
        q = q_all[:, cols]
        k = k_all[:, cols]
        v = v_all[:, cols]
        ck = ck_ref[0, h]
        cv = cv_ref[0, h]
        local = lax.dot_general(q, k, contract, preferred_element_type=jnp.float32) * scale
        allowed = (col <= row) & (valid_ref[0, h] > 0.5)
        local = jnp.where(allowed, local, -1e30)
        memory = lax.dot_general(q, ck, contract, preferred_element_type=jnp.float32) * scale
        top = jnp.maximum(
            jnp.max(local, axis=1, keepdims=True), jnp.max(memory, axis=1, keepdims=True)
        )
        w_local = jnp.exp(local - top)
        w_memory = jnp.exp(memory - top)
        denom = jnp.sum(w_local, axis=1, keepdims=True) + jnp.sum(
            w_memory, axis=1, keepdims=True
        )
        numer = jnp.dot(w_local.astype(v.dtype), v, preferred_element_type=jnp.float32)
        numer = numer + jnp.dot(
            w_memory.astype(cv.dtype), cv, preferred_element_type=jnp.float32
        )
        result = (numer / denom).astype(out_ref.dtype).astype(jnp.float32)
        out_ref[:, :, cols] = result.reshape(sources, depth, head_dim).astype(out_ref.dtype)


def cluster_attention(recv, cent, valid, scale, per_owner, heads_dev):
    sources, _, width = recv.shape
    head_dim = width // heads_dev
    clusters = cent.shape[2]

    def pick(kind):
        return pl.BlockSpec((sources, MOST, width), lambda c: (0, kind * per_owner + c, 0))

    def centroid(kind):
        return pl.BlockSpec((1, heads_dev, clusters, head_dim), lambda c: (kind, 0, 0, 0))

    return pl.pallas_call(
        functools.partial(attention_kernel, scale=scale),
        grid=(per_owner,),
        in_specs=[
            pick(0),
            pick(1),
            pick(2),
            centroid(0),
            centroid(1),
            pl.BlockSpec((1, heads_dev, 1, sources * MOST), lambda c: (c, 0, 0, 0)),
        ],
        out_specs=pl.BlockSpec((sources, MOST, width), lambda c: (0, c, 0)),
        out_shape=jax.ShapeDtypeStruct((sources, per_owner * MOST, width), recv.dtype),
    )(recv, recv, recv, cent, cent, valid)


def on_device(queries, keys, values, clusters, cent_keys, cent_values, out_weight):
    tok_dev, heads_dev, head_dim = queries.shape
    owners = lax.axis_size("seq")
    per_owner = CLUSTERS // owners
    group = per_owner * MOST
    width = heads_dev * head_dim
    cent_rows = 2 * per_owner
    count_rows = 8
    scale = head_dim ** (-0.5)
    dtype = queries.dtype

    assign = clusters[:, :, 0]
    order = jnp.arange(tok_dev, dtype=jnp.int32)
    earlier = (assign[:, :, None] == assign[:, None, :]) & (
        order[None, None, :] < order[None, :, None]
    )
    rank = jnp.sum(earlier.astype(jnp.int32), axis=2)
    slot_of = (assign * MOST + rank).T
    head_cols = jnp.arange(heads_dev, dtype=jnp.int32)[None, :]

    counts = jnp.sum(
        (assign[:, :, None] == jnp.arange(CLUSTERS, dtype=jnp.int32)[None, None, :]).astype(jnp.int32),
        axis=1,
    )
    counts = jnp.transpose(counts.reshape(heads_dev, owners, per_owner), (1, 0, 2))
    counts = counts.reshape(owners, heads_dev * per_owner).astype(dtype)
    counts = jnp.pad(counts, ((0, 0), (0, count_rows * width - heads_dev * per_owner)))
    counts = counts.reshape(owners, count_rows, width)

    cent = jnp.stack([cent_keys, cent_values], axis=0).reshape(cent_rows, width)
    send = place(
        slot_of.T.reshape(heads_dev, 1, tok_dev),
        queries.reshape(tok_dev, width),
        keys.reshape(tok_dev, width),
        values.reshape(tok_dev, width),
        cent,
        counts,
        group,
        min(32, owners),
    )
    recv = lax.all_to_all(send, "seq", split_axis=0, concat_axis=0, tiled=True)

    span = owners * MOST
    cent_in = recv[:, 3 * group : 3 * group + cent_rows].reshape(
        owners, 2, heads_dev, per_owner, head_dim
    )
    cent_in = jnp.transpose(cent_in, (1, 2, 0, 3, 4)).reshape(2, heads_dev, CLUSTERS, head_dim)
    cnt = recv[:, 3 * group + cent_rows, : heads_dev * per_owner].astype(jnp.int32)
    cnt = cnt.reshape(owners, heads_dev, per_owner)
    depth = jnp.arange(MOST, dtype=jnp.int32)
    valid = depth[None, None, None, :] < jnp.transpose(cnt, (2, 1, 0))[..., None]
    valid = valid.astype(jnp.float32).reshape(per_owner, heads_dev, 1, span)

    back = cluster_attention(recv, cent_in, valid, scale, per_owner, heads_dev)
    back = lax.all_to_all(back, "seq", split_axis=0, concat_axis=0, tiled=True)
    back = back.reshape(owners * group, width)
    mixed = project(slot_of, back, out_weight.T, 4)
    return lax.psum_scatter(mixed, "head", scatter_dimension=0, tiled=True)


def solution(mesh):
    return jax.shard_map(
        on_device,
        mesh=mesh,
        in_specs=(
            P("seq", "head", None),
            P("seq", "head", None),
            P("seq", "head", None),
            P("head", "seq", None),
            P("head", "seq", None),
            P("head", "seq", None),
            P("head", None),
        ),
        out_specs=P("head", "seq"),
        check_vma=False,
    )
```
